32 devices in a mesh: groups: 2 (over x), ex: 16 (over z, y, core).
Axes of the slice: x: 2, y: 2, z: 4, core: 2. Of those that a mesh axis runs over, the one named last changes fastest.
Arguments:
- grads: bfloat16 [1024, 65536], P(('groups', 'ex')), parts along dimension 0, may hold values from -6 to 6
- proj: bfloat16 [65536, 1024], P('ex'), may hold values from -0.0234375 to 0.0234375
- target_ids: int32 [24, 128], replicated, may hold values from 0 to 511, as said below
- target_counts: int32 [24], replicated, may hold values from 1 to 128, as said below
Outputs:
- scores: float32 [1024, 24], P(('groups', 'ex')), parts along dimension 0
- sketch: float32 [1024, 1024], P(('groups', 'ex')), parts along dimension 0
The draws below stay inside these ranges and needn't reach their ends.
There are 2 independent parts, one for each index of `groups`. The reference program is written for one: setup_inputs(seed, part) draws one part's arguments, and reference() takes and returns one part's arrays. A program takes and returns all parts, laid end to end along the dimension named above; an argument that names none is the same for every part. Nothing has to cross between parts.
Inputs may be any that keep to these rules, and one draw needn't show every extreme that they name: `target_ids`: indices of examples of this part; slots at or past a domain's count are ignored. `target_counts`: some domain fills all 128 slots.
All inputs are finite; a program needn't handle non-finite values.
Results may differ from the reference program's by a relative error of at most 0.0003.
Values may be sent and summed in bfloat16 or wider, within the bound.
No kernel may reach another device: no remote copies, remote signals or barrier semaphores. Data moves between devices by JAX's collectives and lax.ppermute only.
A program may use at most 128 MiB of HBM per device.

```python
import jax
import jax.numpy as jnp
from jax import lax

G = 65536
K = 1024
DOMAINS = 24
TMAX = 128
EXAMPLES = 512


def draw_target_ids(key, part):
    values = jax.random.randint(key, (DOMAINS, TMAX), 0, EXAMPLES)
    first = jax.random.randint(jax.random.fold_in(key, 3), (), 0, DOMAINS)
    second = jax.random.randint(jax.random.fold_in(key, 5), (), 0, DOMAINS)
    values = values.at[first, 0].set(EXAMPLES - 1)
    values = values.at[second, 1].set(0)
    return values.astype(jnp.int32)


def draw_target_counts(key, part):
    counts = jax.random.randint(key, (DOMAINS,), 2, TMAX + 1)
    filled = jax.random.randint(jax.random.fold_in(key, 7), (), 0, DOMAINS)
    single = jax.random.randint(jax.random.fold_in(key, 9), (), 0, DOMAINS)
    counts = counts.at[single].set(1)
    counts = counts.at[filled].set(TMAX)
    return counts.astype(jnp.int32)


def level_of(rng, extent, pieces, least, top_value):
    def one(position, blocks):
        draws = jax.random.uniform(jax.random.fold_in(jax.random.fold_in(rng, 6), position), (blocks,), jnp.float32, least / len(pieces), top_value / len(pieces))
        return jnp.repeat(jnp.exp(draws), extent[position] // blocks).reshape((-1,) + (1,) * (len(extent) - position - 1))

    factor_of = one(*pieces[0])
    for cut in pieces[1:]:
        factor_of = factor_of * one(*cut)
    return factor_of


def noise(own_key, extent, scale, most, cuts=(), kind=jnp.bfloat16):
    factor_of = level_of(own_key, extent, cuts, -0.22, 0.18) if cuts else 1.0
    drawn = jax.random.normal(own_key, extent, jnp.float32) * scale * factor_of
    return jnp.minimum(jnp.maximum(drawn, -most), most).astype(kind)


def setup_inputs(seed: int = 0, part: int = 0) -> dict:
    splits = jax.random.split(jax.random.key(seed), 5)
    own_keys = jax.random.split(jax.random.fold_in(splits[4], part), 5)
    grads = noise(own_keys[0], (EXAMPLES, G), 1.0, 6.0, ((0, 16),))
    proj = noise(splits[1], (G, K), G ** -0.5, 0.0234375, ((0, 16),))
    target_ids = draw_target_ids(jax.random.fold_in(splits[4], 71), part)
    target_counts = draw_target_counts(jax.random.fold_in(splits[4], 71), part)
    return dict(grads=grads, proj=proj, target_ids=target_ids, target_counts=target_counts)


def reference(grads, proj, target_ids, target_counts):
    sketch = jnp.dot(grads.astype(jnp.float32), proj.astype(jnp.float32), preferred_element_type=jnp.float32)
    gram_matrix = jnp.dot(sketch.T, sketch, precision=lax.Precision.HIGHEST)
    live_slot = jnp.arange(TMAX, dtype=jnp.int32)[None, :] < target_counts[:, None]
    example_index = jnp.arange(EXAMPLES, dtype=jnp.int32)
    matches = (target_ids[:, :, None] == example_index[None, None, :]) & live_slot[:, :, None]
    weight = jnp.sum(matches.astype(jnp.float32), axis=1) / target_counts[:, None].astype(jnp.float32)
    domain = jnp.dot(weight, sketch, precision=lax.Precision.HIGHEST)
    hessian = gram_matrix / jnp.float32(EXAMPLES) + 0.1 * jnp.eye(K, dtype=jnp.float32)
    factor = jnp.linalg.cholesky(hessian)
    middle = lax.linalg.triangular_solve(factor, domain.T, left_side=True, lower=True)
    solved = lax.linalg.triangular_solve(factor, middle, left_side=True, lower=True, transpose_a=True)
    scores = jnp.dot(sketch, solved, precision=lax.Precision.HIGHEST)
    return (scores, sketch)
```

```python
import jax
import jax.numpy as jnp
from jax import lax
from jax.sharding import PartitionSpec as P


def partner(array, axis, bit):
    return lax.ppermute(array, axis, [(i, i ^ 1 << bit) for i in range(lax.axis_size(axis))])


def reduce_scatter(partial_value, bits, position):
    value = partial_value
    for level in range(bits):
        value = value.reshape((-1, 2) + value.shape[1:])
        own_bit = position // 2**level % 2
        kept = lax.dynamic_index_in_dim(value, own_bit, axis=1, keepdims=False)
        sent = lax.dynamic_index_in_dim(value, 1 - own_bit, axis=1, keepdims=False)
        value = kept + partner(sent, "ex", level)
    return value[0]


def all_gather(block, bits, position):
    value = block[None]
    for level in range(bits - 1, -1, -1):
        received = partner(value, "ex", level)
        high_side = position // 2**level % 2 == 1
        low = jnp.where(high_side, received, value)
        high = jnp.where(high_side, value, received)
        value = jnp.stack([low, high], axis=1).reshape((-1,) + value.shape[1:])
    return value


def on_device(grads, proj, target_ids, target_counts):
    count_ex = lax.axis_size("ex")
    bits = count_ex.bit_length() - 1
    position = lax.axis_index("ex")
    ex_rows = grads.shape[0]
    examples = ex_rows * count_ex
    sketch_width = proj.shape[1]
    with jax.named_scope("gradient_exchange"):
        columns = lax.all_to_all(grads, "ex", split_axis=1, concat_axis=0, tiled=True)
    with jax.named_scope("partial_projection"):
        partial_value = jnp.dot(columns, proj, preferred_element_type=jnp.float32)
    with jax.named_scope("sketch_reduce"):
        sketch = reduce_scatter(
            partial_value.reshape(count_ex, ex_rows, sketch_width), bits, position
        )
    with jax.named_scope("sketch_gather"):
        sketch_all = all_gather(sketch, bits, position).reshape(examples, sketch_width)
    slot_count = target_ids.shape[1]
    live_slot = jnp.arange(slot_count, dtype=jnp.int32)[None, :] < target_counts[:, None]
    example_index = jnp.arange(examples, dtype=jnp.int32)
    matches = (target_ids[:, :, None] == example_index[None, None, :]) & live_slot[:, :, None]
    weight = jnp.sum(matches.astype(jnp.float32), axis=1) / target_counts[:, None].astype(
        jnp.float32
    )
    if examples < sketch_width:
        with jax.named_scope("kernel_matrix"):
            kernel = jnp.dot(sketch_all, sketch_all.T, precision=lax.Precision.HIGHEST)
        with jax.named_scope("kernel_solve"):
            system = kernel / jnp.float32(examples) + 0.1 * jnp.eye(examples, dtype=jnp.float32)
            factor = jnp.linalg.cholesky(system)
            middle = lax.linalg.triangular_solve(factor, weight.T, left_side=True, lower=True)
            coeffs = lax.linalg.triangular_solve(
                factor, middle, left_side=True, lower=True, transpose_a=True
            )
        own_kernel = lax.dynamic_slice_in_dim(kernel, position * ex_rows, ex_rows, axis=0)
        scores = jnp.dot(own_kernel, coeffs, precision=lax.Precision.HIGHEST)
    else:
        with jax.named_scope("gram_solve"):
            gram_matrix = jnp.dot(sketch_all.T, sketch_all, precision=lax.Precision.HIGHEST)
            domain = jnp.dot(weight, sketch_all, precision=lax.Precision.HIGHEST)
            hessian = gram_matrix / jnp.float32(examples) + 0.1 * jnp.eye(
                sketch_width, dtype=jnp.float32
            )
            factor = jnp.linalg.cholesky(hessian)
            middle = lax.linalg.triangular_solve(factor, domain.T, left_side=True, lower=True)
            solved = lax.linalg.triangular_solve(
                factor, middle, left_side=True, lower=True, transpose_a=True
            )
        scores = jnp.dot(sketch, solved, precision=lax.Precision.HIGHEST)
    return (scores, sketch)


def solution(mesh):
    placed = (P(("groups", "ex"), None), P("ex", None), P(), P())
    return jax.shard_map(
        on_device,
        mesh=mesh,
        in_specs=placed,
        out_specs=(P(("groups", "ex"), None), P(("groups", "ex"), None)),
        check_vma=False,
    )
```

```python
import jax
import jax.numpy as jnp
from jax import lax
from jax.sharding import PartitionSpec as P
import functools
from jax.experimental import pallas as pl
from jax.experimental.pallas import tpu as pltpu

HI = lax.Precision.HIGHEST

def _invert_block(block):
    size = block.shape[0]
    lane = lax.broadcasted_iota(jnp.int32, block.shape, 1)
    sub = lax.broadcasted_iota(jnp.int32, block.shape, 0)
    lane_row = lax.broadcasted_iota(jnp.int32, (1, size), 1)
    sub_col = lax.broadcasted_iota(jnp.int32, (size, 1), 0)

    def step(k, a):
        row = jnp.sum(jnp.where(sub == k, a, 0.0), axis=0, keepdims=True)
        col = jnp.sum(jnp.where(lane == k, a, 0.0), axis=1, keepdims=True)
        pivot = jnp.sum(jnp.where(lane_row == k, row, 0.0), axis=1, keepdims=True)
        scaled = jnp.where(lane_row == k, 1.0, row) / pivot
        col = jnp.where(sub_col == k, 0.0, col)
        a = jnp.where(lane == k, 0.0, a) - col * scaled
        return jnp.where(sub == k, scaled, a)

    return lax.fori_loop(0, size, step, block)


def _solve_kernel(m_ref, w_ref, y_ref, a_ref, *, block):
    n = m_ref.shape[0]
    a_ref[:, :n] = m_ref[...]
    a_ref[:, n:] = w_ref[...]
    blocks = n // block
    for j in range(blocks):
        lo = j * block
        inverse = _invert_block(a_ref[lo:lo + block, lo:lo + block])
        pivot_rows = jnp.dot(inverse, a_ref[lo:lo + block, lo:], precision=HI,
                             preferred_element_type=jnp.float32)
        for i in range(blocks):
            if i == j:
                continue
            r = i * block
            a_ref[r:r + block, lo:] = a_ref[r:r + block, lo:] - jnp.dot(
                a_ref[r:r + block, lo:lo + block], pivot_rows, precision=HI,
                preferred_element_type=jnp.float32)
        a_ref[lo:lo + block, lo:] = pivot_rows
    y_ref[...] = a_ref[:, n:]


def spd_solve(system, rhs, block=128, interpret=False):
    n = system.shape[0]
    return pl.pallas_call(
        functools.partial(_solve_kernel, block=block),
        out_shape=jax.ShapeDtypeStruct(rhs.shape, jnp.float32),
        scratch_shapes=[pltpu.VMEM((n, n + rhs.shape[1]), jnp.float32)],
        interpret=interpret,
    )(system, rhs)


def partner(array, axis, bit):
    return lax.ppermute(array, axis, [(i, i ^ 1 << bit) for i in range(lax.axis_size(axis))])


def reduce_scatter(partial_value, bits, position):
    value = partial_value
    for level in range(bits):
        value = value.reshape((-1, 2) + value.shape[1:])
        own_bit = position // 2**level % 2
        kept = lax.dynamic_index_in_dim(value, own_bit, axis=1, keepdims=False)
        sent = lax.dynamic_index_in_dim(value, 1 - own_bit, axis=1, keepdims=False)
        value = kept + partner(sent, "ex", level)
    return value[0]


def all_gather(block, bits, position):
    value = block[None]
    for level in range(bits - 1, -1, -1):
        received = partner(value, "ex", level)
        high_side = position // 2**level % 2 == 1
        low = jnp.where(high_side, received, value)
        high = jnp.where(high_side, value, received)
        value = jnp.stack([low, high], axis=1).reshape((-1,) + value.shape[1:])
    return value


def on_device(grads, proj, target_ids, target_counts):
    count_ex = lax.axis_size("ex")
    bits = count_ex.bit_length() - 1
    position = lax.axis_index("ex")
    ex_rows = grads.shape[0]
    examples = ex_rows * count_ex
    sketch_width = proj.shape[1]
    with jax.named_scope("gradient_exchange"):
        columns = lax.all_to_all(grads, "ex", split_axis=1, concat_axis=0, tiled=True)
    with jax.named_scope("partial_projection"):
        partial_value = jnp.dot(columns, proj, preferred_element_type=jnp.float32)
    with jax.named_scope("sketch_reduce"):
        sketch = reduce_scatter(
            partial_value.reshape(count_ex, ex_rows, sketch_width), bits, position
        )
    with jax.named_scope("sketch_gather"):
        sketch_all = all_gather(sketch, bits, position).reshape(examples, sketch_width)
    slot_count = target_ids.shape[1]
    live_slot = jnp.arange(slot_count, dtype=jnp.int32)[None, :] < target_counts[:, None]
    example_index = jnp.arange(examples, dtype=jnp.int32)
    matches = (target_ids[:, :, None] == example_index[None, None, :]) & live_slot[:, :, None]
    weight = jnp.sum(matches.astype(jnp.float32), axis=1) / target_counts[:, None].astype(
        jnp.float32
    )
    if examples < sketch_width and examples % 128 == 0:
        with jax.named_scope("kernel_matrix"):
            kernel = jnp.dot(sketch_all, sketch_all.T, precision=lax.Precision.HIGHEST)
        with jax.named_scope("kernel_solve"):
            system = kernel / jnp.float32(examples) + 0.1 * jnp.eye(examples, dtype=jnp.float32)
            lanes = -(-weight.shape[0] // 128) * 128
            rhs = jnp.pad(weight.T, ((0, 0), (0, lanes - weight.shape[0])))
            coeffs = spd_solve(system, rhs, block=min(128, examples))[:, : weight.shape[0]]
        own_kernel = lax.dynamic_slice_in_dim(kernel, position * ex_rows, ex_rows, axis=0)
        scores = jnp.dot(own_kernel, coeffs, precision=lax.Precision.HIGHEST)
    else:
        with jax.named_scope("gram_solve"):
            gram_matrix = jnp.dot(sketch_all.T, sketch_all, precision=lax.Precision.HIGHEST)
            domain = jnp.dot(weight, sketch_all, precision=lax.Precision.HIGHEST)
            hessian = gram_matrix / jnp.float32(examples) + 0.1 * jnp.eye(
                sketch_width, dtype=jnp.float32
            )
            factor = jnp.linalg.cholesky(hessian)
            middle = lax.linalg.triangular_solve(factor, domain.T, left_side=True, lower=True)
            solved = lax.linalg.triangular_solve(
                factor, middle, left_side=True, lower=True, transpose_a=True
            )
        scores = jnp.dot(sketch, solved, precision=lax.Precision.HIGHEST)
    return (scores, sketch)


def solution(mesh):
    placed = (P(("groups", "ex"), None), P("ex", None), P(), P())
    return jax.shard_map(
        on_device,
        mesh=mesh,
        in_specs=placed,
        out_specs=(P(("groups", "ex"), None), P(("groups", "ex"), None)),
        check_vma=False,
    )
```

```python
import jax
import jax.numpy as jnp
from jax import lax
from jax.sharding import PartitionSpec as P
import functools
from jax.experimental import pallas as pl
from jax.experimental.pallas import tpu as pltpu

HI = lax.Precision.HIGHEST

def _invert_block(block):
    size = block.shape[0]
    lane = lax.broadcasted_iota(jnp.int32, block.shape, 1)
    sub = lax.broadcasted_iota(jnp.int32, block.shape, 0)
    lane_row = lax.broadcasted_iota(jnp.int32, (1, size), 1)
    sub_col = lax.broadcasted_iota(jnp.int32, (size, 1), 0)

    def pick(row, k):
        return jnp.sum(jnp.where(lane_row == k, row, 0.0), axis=1, keepdims=True)

    def step(h, a):
        k = 2 * h
        row0 = jnp.sum(jnp.where(sub == k, a, 0.0), axis=0, keepdims=True)
        row1 = jnp.sum(jnp.where(sub == k + 1, a, 0.0), axis=0, keepdims=True)
        col0 = jnp.sum(jnp.where(lane == k, a, 0.0), axis=1, keepdims=True)
        col1 = jnp.sum(jnp.where(lane == k + 1, a, 0.0), axis=1, keepdims=True)
        p00 = pick(row0, k)
        p01 = pick(row0, k + 1)
        p10 = pick(row1, k)
        p11 = pick(row1, k + 1)
        det = p00 * p11 - p01 * p10
        ident0 = jnp.where(lane_row == k, 1.0, jnp.where(lane_row == k + 1, 0.0, row0))
        ident1 = jnp.where(lane_row == k, 0.0, jnp.where(lane_row == k + 1, 1.0, row1))
        scaled0 = (p11 * ident0 - p01 * ident1) / det
        scaled1 = (p00 * ident1 - p10 * ident0) / det
        pivot_rows = (sub_col == k) | (sub_col == k + 1)
        col0 = jnp.where(pivot_rows, 0.0, col0)
        col1 = jnp.where(pivot_rows, 0.0, col1)
        pivot_cols = (lane == k) | (lane == k + 1)
        a = jnp.where(pivot_cols, 0.0, a) - col0 * scaled0 - col1 * scaled1
        a = jnp.where(sub == k, scaled0, a)
        return jnp.where(sub == k + 1, scaled1, a)

    return lax.fori_loop(0, size // 2, step, block)


def _solve_kernel(m_ref, w_ref, y_ref, a_ref, *, block):
    n = m_ref.shape[0]
    a_ref[:, :n] = m_ref[...]
    a_ref[:, n:] = w_ref[...]
    blocks = n // block
    for j in range(blocks):
        lo = j * block
        inverse = _invert_block(a_ref[lo:lo + block, lo:lo + block])
        pivot_rows = jnp.dot(inverse, a_ref[lo:lo + block, lo:], precision=HI,
                             preferred_element_type=jnp.float32)
        for i in range(blocks):
            if i == j:
                continue
            r = i * block
            a_ref[r:r + block, lo:] = a_ref[r:r + block, lo:] - jnp.dot(
                a_ref[r:r + block, lo:lo + block], pivot_rows, precision=HI,
                preferred_element_type=jnp.float32)
        a_ref[lo:lo + block, lo:] = pivot_rows
    y_ref[...] = a_ref[:, n:]


def spd_solve(system, rhs, block=128, interpret=False):
    n = system.shape[0]
    return pl.pallas_call(
        functools.partial(_solve_kernel, block=block),
        out_shape=jax.ShapeDtypeStruct(rhs.shape, jnp.float32),
        scratch_shapes=[pltpu.VMEM((n, n + rhs.shape[1]), jnp.float32)],
        interpret=interpret,
    )(system, rhs)


def partner(array, axis, bit):
    return lax.ppermute(array, axis, [(i, i ^ 1 << bit) for i in range(lax.axis_size(axis))])


def reduce_scatter(partial_value, bits, position):
    value = partial_value
    for level in range(bits):
        value = value.reshape((-1, 2) + value.shape[1:])
        own_bit = position // 2**level % 2
        kept = lax.dynamic_index_in_dim(value, own_bit, axis=1, keepdims=False)
        sent = lax.dynamic_index_in_dim(value, 1 - own_bit, axis=1, keepdims=False)
        value = kept + partner(sent, "ex", level)
    return value[0]


def all_gather(block, bits, position):
    value = block[None]
    for level in range(bits - 1, -1, -1):
        received = partner(value, "ex", level)
        high_side = position // 2**level % 2 == 1
        low = jnp.where(high_side, received, value)
        high = jnp.where(high_side, value, received)
        value = jnp.stack([low, high], axis=1).reshape((-1,) + value.shape[1:])
    return value


def on_device(grads, proj, target_ids, target_counts):
    count_ex = lax.axis_size("ex")
    bits = count_ex.bit_length() - 1
    position = lax.axis_index("ex")
    ex_rows = grads.shape[0]
    examples = ex_rows * count_ex
    sketch_width = proj.shape[1]
    with jax.named_scope("gradient_exchange"):
        columns = lax.all_to_all(grads, "ex", split_axis=1, concat_axis=0, tiled=True)
    with jax.named_scope("partial_projection"):
        partial_value = jnp.dot(columns, proj, preferred_element_type=jnp.float32)
    with jax.named_scope("sketch_reduce"):
        sketch = reduce_scatter(
            partial_value.reshape(count_ex, ex_rows, sketch_width), bits, position
        )
    with jax.named_scope("sketch_gather"):
        sketch_all = all_gather(sketch, bits, position).reshape(examples, sketch_width)
    slot_count = target_ids.shape[1]
    live_slot = jnp.arange(slot_count, dtype=jnp.int32)[None, :] < target_counts[:, None]
    example_index = jnp.arange(examples, dtype=jnp.int32)
    matches = (target_ids[:, :, None] == example_index[None, None, :]) & live_slot[:, :, None]
    weight = jnp.sum(matches.astype(jnp.float32), axis=1) / target_counts[:, None].astype(
        jnp.float32
    )
    if examples < sketch_width and examples % 128 == 0:
        with jax.named_scope("kernel_matrix"):
            kernel = jnp.dot(sketch_all, sketch_all.T, precision=lax.Precision.HIGHEST)
        with jax.named_scope("kernel_solve"):
            system = kernel / jnp.float32(examples) + 0.1 * jnp.eye(examples, dtype=jnp.float32)
            lanes = -(-weight.shape[0] // 128) * 128
            rhs = jnp.pad(weight.T, ((0, 0), (0, lanes - weight.shape[0])))
            coeffs = spd_solve(system, rhs, block=min(128, examples))[:, : weight.shape[0]]
        own_kernel = lax.dynamic_slice_in_dim(kernel, position * ex_rows, ex_rows, axis=0)
        scores = jnp.dot(own_kernel, coeffs, precision=lax.Precision.HIGHEST)
    else:
        with jax.named_scope("gram_solve"):
            gram_matrix = jnp.dot(sketch_all.T, sketch_all, precision=lax.Precision.HIGHEST)
            domain = jnp.dot(weight, sketch_all, precision=lax.Precision.HIGHEST)
            hessian = gram_matrix / jnp.float32(examples) + 0.1 * jnp.eye(
                sketch_width, dtype=jnp.float32
            )
            factor = jnp.linalg.cholesky(hessian)
            middle = lax.linalg.triangular_solve(factor, domain.T, left_side=True, lower=True)
            solved = lax.linalg.triangular_solve(
                factor, middle, left_side=True, lower=True, transpose_a=True
            )
        scores = jnp.dot(sketch, solved, precision=lax.Precision.HIGHEST)
    return (scores, sketch)


def solution(mesh):
    placed = (P(("groups", "ex"), None), P("ex", None), P(), P())
    return jax.shard_map(
        on_device,
        mesh=mesh,
        in_specs=placed,
        out_specs=(P(("groups", "ex"), None), P(("groups", "ex"), None)),
        check_vma=False,
    )
```

```python
import jax
import jax.numpy as jnp
from jax import lax
from jax.sharding import PartitionSpec as P
import functools
from jax.experimental import pallas as pl
from jax.experimental.pallas import tpu as pltpu

HI = lax.Precision.HIGHEST

def _invert_block(block):
    size = block.shape[0]
    lane = lax.broadcasted_iota(jnp.int32, block.shape, 1)
    sub = lax.broadcasted_iota(jnp.int32, block.shape, 0)
    lane_row = lax.broadcasted_iota(jnp.int32, (1, size), 1)
    sub_col = lax.broadcasted_iota(jnp.int32, (size, 1), 0)

    def pick(row, k):
        return jnp.sum(jnp.where(lane_row == k, row, 0.0), axis=1, keepdims=True)

    def pair_pivot(first, second, k):
        p00 = pick(first, k)
        p01 = pick(first, k + 1)
        p10 = pick(second, k)
        p11 = pick(second, k + 1)
        det = p00 * p11 - p01 * p10
        ident0 = jnp.where(lane_row == k, 1.0, jnp.where(lane_row == k + 1, 0.0, first))
        ident1 = jnp.where(lane_row == k, 0.0, jnp.where(lane_row == k + 1, 1.0, second))
        scaled0 = (p11 * ident0 - p01 * ident1) / det
        scaled1 = (p00 * ident1 - p10 * ident0) / det
        return scaled0, scaled1

    def eliminate(row, k, scaled0, scaled1):
        f0 = pick(row, k)
        f1 = pick(row, k + 1)
        kept = jnp.where((lane_row == k) | (lane_row == k + 1), 0.0, row)
        return kept - f0 * scaled0 - f1 * scaled1

    def step(h, a):
        k = 4 * h
        rows = [jnp.sum(jnp.where(sub == k + t, a, 0.0), axis=0, keepdims=True) for t in range(4)]
        cols = [jnp.sum(jnp.where(lane == k + t, a, 0.0), axis=1, keepdims=True) for t in range(4)]
        s0, s1 = pair_pivot(rows[0], rows[1], k)
        r2 = eliminate(rows[2], k, s0, s1)
        r3 = eliminate(rows[3], k, s0, s1)
        s2, s3 = pair_pivot(r2, r3, k + 2)
        s0 = eliminate(s0, k + 2, s2, s3)
        s1 = eliminate(s1, k + 2, s2, s3)
        slab = (s0, s1, s2, s3)
        pivot_rows = (sub_col >= k) & (sub_col < k + 4)
        a = jnp.where((lane >= k) & (lane < k + 4), 0.0, a)
        for t in range(4):
            a = a - jnp.where(pivot_rows, 0.0, cols[t]) * slab[t]
        for t in range(4):
            a = jnp.where(sub == k + t, slab[t], a)
        return a

    return lax.fori_loop(0, size // 4, step, block)


def _solve_kernel(m_ref, w_ref, y_ref, a_ref, *, block):
    n = m_ref.shape[0]
    a_ref[:, :n] = m_ref[...]
    a_ref[:, n:] = w_ref[...]
    blocks = n // block
    for j in range(blocks):
        lo = j * block
        inverse = _invert_block(a_ref[lo:lo + block, lo:lo + block])
        pivot_rows = jnp.dot(inverse, a_ref[lo:lo + block, lo:], precision=HI,
                             preferred_element_type=jnp.float32)
        for i in range(blocks):
            if i == j:
                continue
            r = i * block
            a_ref[r:r + block, lo:] = a_ref[r:r + block, lo:] - jnp.dot(
                a_ref[r:r + block, lo:lo + block], pivot_rows, precision=HI,
                preferred_element_type=jnp.float32)
        a_ref[lo:lo + block, lo:] = pivot_rows
    y_ref[...] = a_ref[:, n:]


def spd_solve(system, rhs, block=128, interpret=False):
    n = system.shape[0]
    return pl.pallas_call(
        functools.partial(_solve_kernel, block=block),
        out_shape=jax.ShapeDtypeStruct(rhs.shape, jnp.float32),
        scratch_shapes=[pltpu.VMEM((n, n + rhs.shape[1]), jnp.float32)],
        interpret=interpret,
    )(system, rhs)


def partner(array, axis, bit):
    return lax.ppermute(array, axis, [(i, i ^ 1 << bit) for i in range(lax.axis_size(axis))])


def reduce_scatter(partial_value, bits, position):
    value = partial_value
    for level in range(bits):
        value = value.reshape((-1, 2) + value.shape[1:])
        own_bit = position // 2**level % 2
        kept = lax.dynamic_index_in_dim(value, own_bit, axis=1, keepdims=False)
        sent = lax.dynamic_index_in_dim(value, 1 - own_bit, axis=1, keepdims=False)
        value = kept + partner(sent, "ex", level)
    return value[0]


def all_gather(block, bits, position):
    value = block[None]
    for level in range(bits - 1, -1, -1):
        received = partner(value, "ex", level)
        high_side = position // 2**level % 2 == 1
        low = jnp.where(high_side, received, value)
        high = jnp.where(high_side, value, received)
        value = jnp.stack([low, high], axis=1).reshape((-1,) + value.shape[1:])
    return value


def on_device(grads, proj, target_ids, target_counts):
    count_ex = lax.axis_size("ex")
    bits = count_ex.bit_length() - 1
    position = lax.axis_index("ex")
    ex_rows = grads.shape[0]
    examples = ex_rows * count_ex
    sketch_width = proj.shape[1]
    with jax.named_scope("gradient_exchange"):
        columns = lax.all_to_all(grads, "ex", split_axis=1, concat_axis=0, tiled=True)
    with jax.named_scope("partial_projection"):
        partial_value = jnp.dot(columns, proj, preferred_element_type=jnp.float32)
    with jax.named_scope("sketch_reduce"):
        sketch = reduce_scatter(
            partial_value.reshape(count_ex, ex_rows, sketch_width), bits, position
        )
    with jax.named_scope("sketch_gather"):
        sketch_all = all_gather(sketch, bits, position).reshape(examples, sketch_width)
    slot_count = target_ids.shape[1]
    live_slot = jnp.arange(slot_count, dtype=jnp.int32)[None, :] < target_counts[:, None]
    example_index = jnp.arange(examples, dtype=jnp.int32)
    matches = (target_ids[:, :, None] == example_index[None, None, :]) & live_slot[:, :, None]
    weight = jnp.sum(matches.astype(jnp.float32), axis=1) / target_counts[:, None].astype(
        jnp.float32
    )
    if examples < sketch_width and examples % 128 == 0:
        with jax.named_scope("kernel_matrix"):
            kernel = jnp.dot(sketch_all, sketch_all.T, precision=lax.Precision.HIGHEST)
        with jax.named_scope("kernel_solve"):
            system = kernel / jnp.float32(examples) + 0.1 * jnp.eye(examples, dtype=jnp.float32)
            lanes = -(-weight.shape[0] // 128) * 128
            rhs = jnp.pad(weight.T, ((0, 0), (0, lanes - weight.shape[0])))
            coeffs = spd_solve(system, rhs, block=min(128, examples))[:, : weight.shape[0]]
        own_kernel = lax.dynamic_slice_in_dim(kernel, position * ex_rows, ex_rows, axis=0)
        scores = jnp.dot(own_kernel, coeffs, precision=lax.Precision.HIGHEST)
    else:
        with jax.named_scope("gram_solve"):
            gram_matrix = jnp.dot(sketch_all.T, sketch_all, precision=lax.Precision.HIGHEST)
            domain = jnp.dot(weight, sketch_all, precision=lax.Precision.HIGHEST)
            hessian = gram_matrix / jnp.float32(examples) + 0.1 * jnp.eye(
                sketch_width, dtype=jnp.float32
            )
            factor = jnp.linalg.cholesky(hessian)
            middle = lax.linalg.triangular_solve(factor, domain.T, left_side=True, lower=True)
            solved = lax.linalg.triangular_solve(
                factor, middle, left_side=True, lower=True, transpose_a=True
            )
        scores = jnp.dot(sketch, solved, precision=lax.Precision.HIGHEST)
    return (scores, sketch)


def solution(mesh):
    placed = (P(("groups", "ex"), None), P("ex", None), P(), P())
    return jax.shard_map(
        on_device,
        mesh=mesh,
        in_specs=placed,
        out_specs=(P(("groups", "ex"), None), P(("groups", "ex"), None)),
        check_vma=False,
    )
```

```python
import jax
import jax.numpy as jnp
from jax import lax
from jax.sharding import PartitionSpec as P
import functools
from jax.experimental import pallas as pl
from jax.experimental.pallas import tpu as pltpu

HI = lax.Precision.HIGHEST

def _invert_block(block):
    size = block.shape[0]
    lane = lax.broadcasted_iota(jnp.int32, block.shape, 1)
    sub = lax.broadcasted_iota(jnp.int32, block.shape, 0)
    lane_row = lax.broadcasted_iota(jnp.int32, (1, size), 1)
    sub_col = lax.broadcasted_iota(jnp.int32, (size, 1), 0)

    def pick(row, k):
        return jnp.sum(jnp.where(lane_row == k, row, 0.0), axis=1, keepdims=True)

    def pair_pivot(first, second, k):
        p00 = pick(first, k)
        p01 = pick(first, k + 1)
        p10 = pick(second, k)
        p11 = pick(second, k + 1)
        det = p00 * p11 - p01 * p10
        ident0 = jnp.where(lane_row == k, 1.0, jnp.where(lane_row == k + 1, 0.0, first))
        ident1 = jnp.where(lane_row == k, 0.0, jnp.where(lane_row == k + 1, 1.0, second))
        scaled0 = (p11 * ident0 - p01 * ident1) / det
        scaled1 = (p00 * ident1 - p10 * ident0) / det
        return scaled0, scaled1

    def eliminate(row, k, scaled0, scaled1):
        f0 = pick(row, k)
        f1 = pick(row, k + 1)
        kept = jnp.where((lane_row == k) | (lane_row == k + 1), 0.0, row)
        return kept - f0 * scaled0 - f1 * scaled1

    def step(h, a):
        k = 4 * h
        rows = [jnp.sum(jnp.where(sub == k + t, a, 0.0), axis=0, keepdims=True) for t in range(4)]
        cols = [jnp.sum(jnp.where(lane == k + t, a, 0.0), axis=1, keepdims=True) for t in range(4)]
        s0, s1 = pair_pivot(rows[0], rows[1], k)
        r2 = eliminate(rows[2], k, s0, s1)
        r3 = eliminate(rows[3], k, s0, s1)
        s2, s3 = pair_pivot(r2, r3, k + 2)
        s0 = eliminate(s0, k + 2, s2, s3)
        s1 = eliminate(s1, k + 2, s2, s3)
        slab = (s0, s1, s2, s3)
        pivot_rows = (sub_col >= k) & (sub_col < k + 4)
        a = jnp.where((lane >= k) & (lane < k + 4), 0.0, a)
        for t in range(4):
            a = a - jnp.where(pivot_rows, 0.0, cols[t]) * slab[t]
        for t in range(4):
            a = jnp.where(sub == k + t, slab[t], a)
        return a

    return lax.fori_loop(0, size // 4, step, block)


def _solve_kernel(m_ref, w_ref, y_ref, a_ref, *, block):
    n = m_ref.shape[0]
    a_ref[:, :n] = m_ref[...]
    a_ref[:, n:] = w_ref[...]
    blocks = n // block
    for j in range(blocks):
        lo = j * block
        inverse = _invert_block(a_ref[lo:lo + block, lo:lo + block])
        pivot_rows = jnp.dot(inverse, a_ref[lo:lo + block, lo:], precision=HI,
                             preferred_element_type=jnp.float32)
        for i in range(blocks):
            if i == j:
                continue
            r = i * block
            a_ref[r:r + block, lo:] = a_ref[r:r + block, lo:] - jnp.dot(
                a_ref[r:r + block, lo:lo + block], pivot_rows, precision=HI,
                preferred_element_type=jnp.float32)
        a_ref[lo:lo + block, lo:] = pivot_rows
    y_ref[...] = a_ref[:, n:]


def spd_solve(system, rhs, block=128, interpret=False):
    n = system.shape[0]
    return pl.pallas_call(
        functools.partial(_solve_kernel, block=block),
        out_shape=jax.ShapeDtypeStruct(rhs.shape, jnp.float32),
        scratch_shapes=[pltpu.VMEM((n, n + rhs.shape[1]), jnp.float32)],
        interpret=interpret,
    )(system, rhs)


def partner(array, axis, bit):
    return lax.ppermute(array, axis, [(i, i ^ 1 << bit) for i in range(lax.axis_size(axis))])


def reduce_scatter(partial_value, order, position):
    bits = len(order)
    value = partial_value.reshape((2,) * bits + partial_value.shape[1:])
    remaining = list(range(bits - 1, -1, -1))
    for level in order:
        axis = remaining.index(level)
        own_bit = position // 2**level % 2
        kept = lax.dynamic_index_in_dim(value, own_bit, axis=axis, keepdims=False)
        sent = lax.dynamic_index_in_dim(value, 1 - own_bit, axis=axis, keepdims=False)
        value = kept + partner(sent, "ex", level)
        remaining.remove(level)
    return value


def all_gather(block, order, position):
    value = block
    present = []
    for level in reversed(order):
        received = partner(value, "ex", level)
        high_side = position // 2**level % 2 == 1
        low = jnp.where(high_side, received, value)
        high = jnp.where(high_side, value, received)
        present.append(level)
        present.sort(reverse=True)
        value = jnp.stack([low, high], axis=present.index(level))
    return value.reshape((-1,) + block.shape[1:])


def bit_orders(bits):
    first = list(range(bits))
    if bits < 3:
        return [first]
    return [first, [0, 2, 1] + list(range(3, bits))]


def on_device(grads, proj, target_ids, target_counts):
    count_ex = lax.axis_size("ex")
    bits = count_ex.bit_length() - 1
    position = lax.axis_index("ex")
    ex_rows = grads.shape[0]
    examples = ex_rows * count_ex
    sketch_width = proj.shape[1]
    with jax.named_scope("gradient_exchange"):
        columns = lax.all_to_all(grads, "ex", split_axis=1, concat_axis=0, tiled=True)
    with jax.named_scope("partial_projection"):
        partial_value = jnp.dot(columns, proj, preferred_element_type=jnp.float32)
    orders = bit_orders(bits)
    width = sketch_width // len(orders)
    owned, gathered = [], []
    for half, order in enumerate(orders):
        with jax.named_scope("sketch_reduce"):
            part = reduce_scatter(
                partial_value[:, half * width:(half + 1) * width].reshape(
                    count_ex, ex_rows, width
                ),
                order,
                position,
            )
        with jax.named_scope("sketch_gather"):
            gathered.append(all_gather(part, order, position))
        owned.append(part)
    sketch = jnp.concatenate(owned, axis=1)
    sketch_all = jnp.concatenate(gathered, axis=1)
    slot_count = target_ids.shape[1]
    live_slot = jnp.arange(slot_count, dtype=jnp.int32)[None, :] < target_counts[:, None]
    example_index = jnp.arange(examples, dtype=jnp.int32)
    matches = (target_ids[:, :, None] == example_index[None, None, :]) & live_slot[:, :, None]
    weight = jnp.sum(matches.astype(jnp.float32), axis=1) / target_counts[:, None].astype(
        jnp.float32
    )
    if examples < sketch_width and examples % 128 == 0:
        with jax.named_scope("kernel_matrix"):
            kernel = jnp.dot(sketch_all, sketch_all.T, precision=lax.Precision.HIGHEST)
        with jax.named_scope("kernel_solve"):
            system = kernel / jnp.float32(examples) + 0.1 * jnp.eye(examples, dtype=jnp.float32)
            lanes = -(-weight.shape[0] // 128) * 128
            rhs = jnp.pad(weight.T, ((0, 0), (0, lanes - weight.shape[0])))
            coeffs = spd_solve(system, rhs, block=min(128, examples))[:, : weight.shape[0]]
        own_kernel = lax.dynamic_slice_in_dim(kernel, position * ex_rows, ex_rows, axis=0)
        scores = jnp.dot(own_kernel, coeffs, precision=lax.Precision.HIGHEST)
    else:
        with jax.named_scope("gram_solve"):
            gram_matrix = jnp.dot(sketch_all.T, sketch_all, precision=lax.Precision.HIGHEST)
            domain = jnp.dot(weight, sketch_all, precision=lax.Precision.HIGHEST)
            hessian = gram_matrix / jnp.float32(examples) + 0.1 * jnp.eye(
                sketch_width, dtype=jnp.float32
            )
            factor = jnp.linalg.cholesky(hessian)
            middle = lax.linalg.triangular_solve(factor, domain.T, left_side=True, lower=True)
            solved = lax.linalg.triangular_solve(
                factor, middle, left_side=True, lower=True, transpose_a=True
            )
        scores = jnp.dot(sketch, solved, precision=lax.Precision.HIGHEST)
    return (scores, sketch)


def solution(mesh):
    placed = (P(("groups", "ex"), None), P("ex", None), P(), P())
    return jax.shard_map(
        on_device,
        mesh=mesh,
        in_specs=placed,
        out_specs=(P(("groups", "ex"), None), P(("groups", "ex"), None)),
        check_vma=False,
    )
```

```python
import jax
import jax.numpy as jnp
from jax import lax
from jax.sharding import PartitionSpec as P
import functools
from jax.experimental import pallas as pl
from jax.experimental.pallas import tpu as pltpu

HI = lax.Precision.HIGHEST

def _invert_block(block):
    size = block.shape[0]
    lane = lax.broadcasted_iota(jnp.int32, block.shape, 1)
    sub = lax.broadcasted_iota(jnp.int32, block.shape, 0)
    lane_row = lax.broadcasted_iota(jnp.int32, (1, size), 1)
    sub_col = lax.broadcasted_iota(jnp.int32, (size, 1), 0)

    def pick(row, k):
        return jnp.sum(jnp.where(lane_row == k, row, 0.0), axis=1, keepdims=True)

    def pair_pivot(first, second, k):
        p00 = pick(first, k)
        p01 = pick(first, k + 1)
        p10 = pick(second, k)
        p11 = pick(second, k + 1)
        det = p00 * p11 - p01 * p10
        ident0 = jnp.where(lane_row == k, 1.0, jnp.where(lane_row == k + 1, 0.0, first))
        ident1 = jnp.where(lane_row == k, 0.0, jnp.where(lane_row == k + 1, 1.0, second))
        scaled0 = (p11 * ident0 - p01 * ident1) / det
        scaled1 = (p00 * ident1 - p10 * ident0) / det
        return scaled0, scaled1

    def eliminate(row, k, scaled0, scaled1):
        f0 = pick(row, k)
        f1 = pick(row, k + 1)
        kept = jnp.where((lane_row == k) | (lane_row == k + 1), 0.0, row)
        return kept - f0 * scaled0 - f1 * scaled1

    def step(h, a):
        k = 4 * h
        rows = [jnp.sum(jnp.where(sub == k + t, a, 0.0), axis=0, keepdims=True) for t in range(4)]
        cols = [jnp.sum(jnp.where(lane == k + t, a, 0.0), axis=1, keepdims=True) for t in range(4)]
        s0, s1 = pair_pivot(rows[0], rows[1], k)
        r2 = eliminate(rows[2], k, s0, s1)
        r3 = eliminate(rows[3], k, s0, s1)
        s2, s3 = pair_pivot(r2, r3, k + 2)
        s0 = eliminate(s0, k + 2, s2, s3)
        s1 = eliminate(s1, k + 2, s2, s3)
        slab = (s0, s1, s2, s3)
        pivot_rows = (sub_col >= k) & (sub_col < k + 4)
        a = jnp.where((lane >= k) & (lane < k + 4), 0.0, a)
        for t in range(4):
            a = a - jnp.where(pivot_rows, 0.0, cols[t]) * slab[t]
        for t in range(4):
            a = jnp.where(sub == k + t, slab[t], a)
        return a

    return lax.fori_loop(0, size // 4, step, block)


def _solve_kernel(m_ref, w_ref, y_ref, a_ref, *, block):
    n = m_ref.shape[0]
    a_ref[:, :n] = m_ref[...]
    a_ref[:, n:] = w_ref[...]
    blocks = n // block
    for j in range(blocks):
        lo = j * block
        inverse = _invert_block(a_ref[lo:lo + block, lo:lo + block])
        pivot_rows = jnp.dot(inverse, a_ref[lo:lo + block, lo:], precision=HI,
                             preferred_element_type=jnp.float32)
        for i in range(blocks):
            if i == j:
                continue
            r = i * block
            a_ref[r:r + block, lo:] = a_ref[r:r + block, lo:] - jnp.dot(
                a_ref[r:r + block, lo:lo + block], pivot_rows, precision=HI,
                preferred_element_type=jnp.float32)
        a_ref[lo:lo + block, lo:] = pivot_rows
    y_ref[...] = a_ref[:, n:]


def spd_solve(system, rhs, block=128, interpret=False):
    n = system.shape[0]
    return pl.pallas_call(
        functools.partial(_solve_kernel, block=block),
        out_shape=jax.ShapeDtypeStruct(rhs.shape, jnp.float32),
        scratch_shapes=[pltpu.VMEM((n, n + rhs.shape[1]), jnp.float32)],
        interpret=interpret,
    )(system, rhs)


def partner(array, axis, bit):
    return lax.ppermute(array, axis, [(i, i ^ 1 << bit) for i in range(lax.axis_size(axis))])


def reduce_scatter(partial_value, order, position):
    bits = len(order)
    value = partial_value.reshape((2,) * bits + partial_value.shape[1:])
    remaining = list(range(bits - 1, -1, -1))
    for level in order:
        axis = remaining.index(level)
        own_bit = position // 2**level % 2
        kept = lax.dynamic_index_in_dim(value, own_bit, axis=axis, keepdims=False)
        sent = lax.dynamic_index_in_dim(value, 1 - own_bit, axis=axis, keepdims=False)
        value = kept + partner(sent, "ex", level)
        remaining.remove(level)
    return value


def all_gather(block, order, position):
    value = block
    present = []
    for level in reversed(order):
        received = partner(value, "ex", level)
        high_side = position // 2**level % 2 == 1
        low = jnp.where(high_side, received, value)
        high = jnp.where(high_side, value, received)
        present.append(level)
        present.sort(reverse=True)
        value = jnp.stack([low, high], axis=present.index(level))
    return value.reshape((-1,) + block.shape[1:])


def bit_orders(bits):
    first = list(range(bits))
    if bits < 3:
        return [first]
    return [first, [0, 2, 1] + list(range(3, bits))]


def on_device(grads, proj, target_ids, target_counts):
    count_ex = lax.axis_size("ex")
    bits = count_ex.bit_length() - 1
    position = lax.axis_index("ex")
    ex_rows = grads.shape[0]
    examples = ex_rows * count_ex
    sketch_width = proj.shape[1]
    with jax.named_scope("gradient_exchange"):
        columns = lax.all_to_all(grads, "ex", split_axis=1, concat_axis=0, tiled=True)
    orders = bit_orders(bits)
    width = sketch_width // len(orders)
    owned, gathered = [], []
    for half, order in enumerate(orders):
        with jax.named_scope("partial_projection"):
            partial_value = jnp.dot(
                columns, proj[:, half * width:(half + 1) * width],
                preferred_element_type=jnp.float32,
            )
        with jax.named_scope("sketch_reduce"):
            part = reduce_scatter(
                partial_value.reshape(count_ex, ex_rows, width),
                order,
                position,
            )
        with jax.named_scope("sketch_gather"):
            gathered.append(all_gather(part, order, position))
        owned.append(part)
    sketch = jnp.concatenate(owned, axis=1)
    sketch_all = jnp.concatenate(gathered, axis=1)
    slot_count = target_ids.shape[1]
    live_slot = jnp.arange(slot_count, dtype=jnp.int32)[None, :] < target_counts[:, None]
    example_index = jnp.arange(examples, dtype=jnp.int32)
    matches = (target_ids[:, :, None] == example_index[None, None, :]) & live_slot[:, :, None]
    weight = jnp.sum(matches.astype(jnp.float32), axis=1) / target_counts[:, None].astype(
        jnp.float32
    )
    if examples < sketch_width and examples % 128 == 0:
        with jax.named_scope("kernel_matrix"):
            kernel = jnp.dot(sketch_all, sketch_all.T, precision=lax.Precision.HIGHEST)
        with jax.named_scope("kernel_solve"):
            system = kernel / jnp.float32(examples) + 0.1 * jnp.eye(examples, dtype=jnp.float32)
            lanes = -(-weight.shape[0] // 128) * 128
            rhs = jnp.pad(weight.T, ((0, 0), (0, lanes - weight.shape[0])))
            coeffs = spd_solve(system, rhs, block=min(128, examples))[:, : weight.shape[0]]
        own_kernel = lax.dynamic_slice_in_dim(kernel, position * ex_rows, ex_rows, axis=0)
        scores = jnp.dot(own_kernel, coeffs, precision=lax.Precision.HIGHEST)
    else:
        with jax.named_scope("gram_solve"):
            gram_matrix = jnp.dot(sketch_all.T, sketch_all, precision=lax.Precision.HIGHEST)
            domain = jnp.dot(weight, sketch_all, precision=lax.Precision.HIGHEST)
            hessian = gram_matrix / jnp.float32(examples) + 0.1 * jnp.eye(
                sketch_width, dtype=jnp.float32
            )
            factor = jnp.linalg.cholesky(hessian)
            middle = lax.linalg.triangular_solve(factor, domain.T, left_side=True, lower=True)
            solved = lax.linalg.triangular_solve(
                factor, middle, left_side=True, lower=True, transpose_a=True
            )
        scores = jnp.dot(sketch, solved, precision=lax.Precision.HIGHEST)
    return (scores, sketch)


def solution(mesh):
    placed = (P(("groups", "ex"), None), P("ex", None), P(), P())
    return jax.shard_map(
        on_device,
        mesh=mesh,
        in_specs=placed,
        out_specs=(P(("groups", "ex"), None), P(("groups", "ex"), None)),
        check_vma=False,
    )
```

```python
import jax
import jax.numpy as jnp
from jax import lax
from jax.sharding import PartitionSpec as P
import functools
from jax.experimental import pallas as pl
from jax.experimental.pallas import tpu as pltpu

HI = lax.Precision.HIGHEST

def _invert_block(block):
    size = block.shape[0]
    lane = lax.broadcasted_iota(jnp.int32, block.shape, 1)
    sub = lax.broadcasted_iota(jnp.int32, block.shape, 0)
    lane_row = lax.broadcasted_iota(jnp.int32, (1, size), 1)
    sub_col = lax.broadcasted_iota(jnp.int32, (size, 1), 0)

    def pick(row, k):
        return jnp.sum(jnp.where(lane_row == k, row, 0.0), axis=1, keepdims=True)

    def pair_pivot(first, second, k):
        p00 = pick(first, k)
        p01 = pick(first, k + 1)
        p10 = pick(second, k)
        p11 = pick(second, k + 1)
        det = p00 * p11 - p01 * p10
        ident0 = jnp.where(lane_row == k, 1.0, jnp.where(lane_row == k + 1, 0.0, first))
        ident1 = jnp.where(lane_row == k, 0.0, jnp.where(lane_row == k + 1, 1.0, second))
        scaled0 = (p11 * ident0 - p01 * ident1) / det
        scaled1 = (p00 * ident1 - p10 * ident0) / det
        return scaled0, scaled1

    def eliminate(row, k, scaled0, scaled1):
        f0 = pick(row, k)
        f1 = pick(row, k + 1)
        kept = jnp.where((lane_row == k) | (lane_row == k + 1), 0.0, row)
        return kept - f0 * scaled0 - f1 * scaled1

    def step(h, a):
        k = 4 * h
        base = k - k % 8
        tile = jnp.sum(
            jnp.where((sub >= base) & (sub < base + 8), a, 0.0).reshape(size // 8, 8, size), axis=0)
        in_tile = lax.broadcasted_iota(jnp.int32, (8, size), 0)
        rows = [jnp.sum(jnp.where(in_tile == k % 8 + t, tile, 0.0), axis=0, keepdims=True)
                for t in range(4)]
        cols = [jnp.sum(jnp.where(lane == k + t, a, 0.0), axis=1, keepdims=True) for t in range(4)]
        s0, s1 = pair_pivot(rows[0], rows[1], k)
        r2 = eliminate(rows[2], k, s0, s1)
        r3 = eliminate(rows[3], k, s0, s1)
        s2, s3 = pair_pivot(r2, r3, k + 2)
        s0 = eliminate(s0, k + 2, s2, s3)
        s1 = eliminate(s1, k + 2, s2, s3)
        slab = (s0, s1, s2, s3)
        pivot_rows = (sub_col >= k) & (sub_col < k + 4)
        a = jnp.where((lane >= k) & (lane < k + 4), 0.0, a)
        for t in range(4):
            a = a - jnp.where(pivot_rows, 0.0, cols[t]) * slab[t]
        for t in range(4):
            a = jnp.where(sub == k + t, slab[t], a)
        return a

    return lax.fori_loop(0, size // 4, step, block)


def _solve_kernel(m_ref, w_ref, y_ref, a_ref, *, block):
    n = m_ref.shape[0]
    a_ref[:, :n] = m_ref[...]
    a_ref[:, n:] = w_ref[...]
    blocks = n // block
    for j in range(blocks):
        lo = j * block
        hi = lo + block
        inverse = _invert_block(a_ref[lo:hi, lo:hi])
        pivot_rows = jnp.dot(inverse, a_ref[lo:hi, hi:], precision=HI,
                             preferred_element_type=jnp.float32)
        for i in range(blocks):
            if i == j:
                continue
            r = i * block
            a_ref[r:r + block, hi:] = a_ref[r:r + block, hi:] - jnp.dot(
                a_ref[r:r + block, lo:hi], pivot_rows, precision=HI,
                preferred_element_type=jnp.float32)
        a_ref[lo:hi, hi:] = pivot_rows
    y_ref[...] = a_ref[:, n:]


def spd_solve(system, rhs, block=128, interpret=False):
    n = system.shape[0]
    return pl.pallas_call(
        functools.partial(_solve_kernel, block=block),
        out_shape=jax.ShapeDtypeStruct(rhs.shape, jnp.float32),
        scratch_shapes=[pltpu.VMEM((n, n + rhs.shape[1]), jnp.float32)],
        interpret=interpret,
    )(system, rhs)


def partner(array, axis, bit):
    return lax.ppermute(array, axis, [(i, i ^ 1 << bit) for i in range(lax.axis_size(axis))])


def reduce_scatter(partial_value, order, position):
    bits = len(order)
    value = partial_value.reshape((2,) * bits + partial_value.shape[1:])
    remaining = list(range(bits - 1, -1, -1))
    for level in order:
        axis = remaining.index(level)
        own_bit = position // 2**level % 2
        kept = lax.dynamic_index_in_dim(value, own_bit, axis=axis, keepdims=False)
        sent = lax.dynamic_index_in_dim(value, 1 - own_bit, axis=axis, keepdims=False)
        value = kept + partner(sent, "ex", level)
        remaining.remove(level)
    return value


def all_gather(block, order, position):
    value = block
    present = []
    for level in reversed(order):
        received = partner(value, "ex", level)
        high_side = position // 2**level % 2 == 1
        low = jnp.where(high_side, received, value)
        high = jnp.where(high_side, value, received)
        present.append(level)
        present.sort(reverse=True)
        value = jnp.stack([low, high], axis=present.index(level))
    return value.reshape((-1,) + block.shape[1:])


def bit_orders(bits):
    first = list(range(bits))
    if bits < 3:
        return [first]
    return [first, [0, 2, 1] + list(range(3, bits))]


def on_device(grads, proj, target_ids, target_counts):
    count_ex = lax.axis_size("ex")
    bits = count_ex.bit_length() - 1
    position = lax.axis_index("ex")
    ex_rows = grads.shape[0]
    examples = ex_rows * count_ex
    sketch_width = proj.shape[1]
    with jax.named_scope("gradient_exchange"):
        columns = lax.all_to_all(grads, "ex", split_axis=1, concat_axis=0, tiled=True)
    with jax.named_scope("partial_projection"):
        partial_value = jnp.dot(columns, proj, preferred_element_type=jnp.float32)
    orders = bit_orders(bits)
    width = sketch_width // len(orders)
    owned, gathered = [], []
    for half, order in enumerate(orders):
        with jax.named_scope("sketch_reduce"):
            part = reduce_scatter(
                partial_value[:, half * width:(half + 1) * width].reshape(
                    count_ex, ex_rows, width
                ),
                order,
                position,
            )
        with jax.named_scope("sketch_gather"):
            gathered.append(all_gather(part, order, position))
        owned.append(part)
    sketch = jnp.concatenate(owned, axis=1)
    sketch_all = jnp.concatenate(gathered, axis=1)
    slot_count = target_ids.shape[1]
    live_slot = jnp.arange(slot_count, dtype=jnp.int32)[None, :] < target_counts[:, None]
    example_index = jnp.arange(examples, dtype=jnp.int32)
    matches = (target_ids[:, :, None] == example_index[None, None, :]) & live_slot[:, :, None]
    weight = jnp.sum(matches.astype(jnp.float32), axis=1) / target_counts[:, None].astype(
        jnp.float32
    )
    if examples < sketch_width and examples % 128 == 0:
        with jax.named_scope("kernel_matrix"):
            kernel = jnp.dot(sketch_all, sketch_all.T, precision=lax.Precision.HIGHEST)
        with jax.named_scope("kernel_solve"):
            system = kernel / jnp.float32(examples) + 0.1 * jnp.eye(examples, dtype=jnp.float32)
            lanes = -(-weight.shape[0] // 128) * 128
            rhs = jnp.pad(weight.T, ((0, 0), (0, lanes - weight.shape[0])))
            coeffs = spd_solve(system, rhs, block=min(128, examples))[:, : weight.shape[0]]
        own_kernel = lax.dynamic_slice_in_dim(kernel, position * ex_rows, ex_rows, axis=0)
        scores = jnp.dot(own_kernel, coeffs, precision=lax.Precision.HIGHEST)
    else:
        with jax.named_scope("gram_solve"):
            gram_matrix = jnp.dot(sketch_all.T, sketch_all, precision=lax.Precision.HIGHEST)
            domain = jnp.dot(weight, sketch_all, precision=lax.Precision.HIGHEST)
            hessian = gram_matrix / jnp.float32(examples) + 0.1 * jnp.eye(
                sketch_width, dtype=jnp.float32
            )
            factor = jnp.linalg.cholesky(hessian)
            middle = lax.linalg.triangular_solve(factor, domain.T, left_side=True, lower=True)
            solved = lax.linalg.triangular_solve(
                factor, middle, left_side=True, lower=True, transpose_a=True
            )
        scores = jnp.dot(sketch, solved, precision=lax.Precision.HIGHEST)
    return (scores, sketch)


def solution(mesh):
    placed = (P(("groups", "ex"), None), P("ex", None), P(), P())
    return jax.shard_map(
        on_device,
        mesh=mesh,
        in_specs=placed,
        out_specs=(P(("groups", "ex"), None), P(("groups", "ex"), None)),
        check_vma=False,
    )
```

```python
import jax
import jax.numpy as jnp
from jax import lax
from jax.sharding import PartitionSpec as P
import functools
from jax.experimental import pallas as pl
from jax.experimental.pallas import tpu as pltpu

HI = lax.Precision.HIGHEST

def _invert_block(block):
    size = block.shape[0]
    lane = lax.broadcasted_iota(jnp.int32, block.shape, 1)
    sub = lax.broadcasted_iota(jnp.int32, block.shape, 0)
    lane_row = lax.broadcasted_iota(jnp.int32, (1, size), 1)
    sub_col = lax.broadcasted_iota(jnp.int32, (size, 1), 0)

    def pick(row, k):
        return jnp.sum(jnp.where(lane_row == k, row, 0.0), axis=1, keepdims=True)

    def pair_pivot(first, second, k):
        p00 = pick(first, k)
        p01 = pick(first, k + 1)
        p10 = pick(second, k)
        p11 = pick(second, k + 1)
        det = p00 * p11 - p01 * p10
        ident0 = jnp.where(lane_row == k, 1.0, jnp.where(lane_row == k + 1, 0.0, first))
        ident1 = jnp.where(lane_row == k, 0.0, jnp.where(lane_row == k + 1, 1.0, second))
        scaled0 = (p11 * ident0 - p01 * ident1) / det
        scaled1 = (p00 * ident1 - p10 * ident0) / det
        return scaled0, scaled1

    def eliminate(row, k, scaled0, scaled1):
        f0 = pick(row, k)
        f1 = pick(row, k + 1)
        kept = jnp.where((lane_row == k) | (lane_row == k + 1), 0.0, row)
        return kept - f0 * scaled0 - f1 * scaled1

    def step(h, a):
        k = 4 * h
        base = k - k % 8
        tile = jnp.sum(
            jnp.where((sub >= base) & (sub < base + 8), a, 0.0).reshape(size // 8, 8, size), axis=0)
        in_tile = lax.broadcasted_iota(jnp.int32, (8, size), 0)
        rows = [jnp.sum(jnp.where(in_tile == k % 8 + t, tile, 0.0), axis=0, keepdims=True)
                for t in range(4)]
        cols = [jnp.sum(jnp.where(lane == k + t, a, 0.0), axis=1, keepdims=True) for t in range(4)]
        s0, s1 = pair_pivot(rows[0], rows[1], k)
        r2 = eliminate(rows[2], k, s0, s1)
        r3 = eliminate(rows[3], k, s0, s1)
        s2, s3 = pair_pivot(r2, r3, k + 2)
        s0 = eliminate(s0, k + 2, s2, s3)
        s1 = eliminate(s1, k + 2, s2, s3)
        slab = (s0, s1, s2, s3)
        pivot_rows = (sub_col >= k) & (sub_col < k + 4)
        a = jnp.where((lane >= k) & (lane < k + 4), 0.0, a)
        for t in range(4):
            a = a - jnp.where(pivot_rows, 0.0, cols[t]) * slab[t]
        for t in range(4):
            a = jnp.where(sub == k + t, slab[t], a)
        return a

    return lax.fori_loop(0, size // 4, step, block)


def _solve_kernel(m_ref, w_ref, y_ref, a_ref, *, block):
    n = m_ref.shape[0]
    a_ref[:, :n] = m_ref[...]
    a_ref[:, n:] = w_ref[...]
    blocks = n // block
    for j in range(blocks):
        lo = j * block
        hi = lo + block
        inverse = _invert_block(a_ref[lo:hi, lo:hi])
        pivot_rows = jnp.dot(inverse, a_ref[lo:hi, hi:], precision=HI,
                             preferred_element_type=jnp.float32)
        for i in range(blocks):
            if i == j:
                continue
            r = i * block
            a_ref[r:r + block, hi:] = a_ref[r:r + block, hi:] - jnp.dot(
                a_ref[r:r + block, lo:hi], pivot_rows, precision=HI,
                preferred_element_type=jnp.float32)
        a_ref[lo:hi, hi:] = pivot_rows
    y_ref[...] = a_ref[:, n:]


def spd_solve(system, rhs, block=128, interpret=False):
    n = system.shape[0]
    return pl.pallas_call(
        functools.partial(_solve_kernel, block=block),
        out_shape=jax.ShapeDtypeStruct(rhs.shape, jnp.float32),
        scratch_shapes=[pltpu.VMEM((n, n + rhs.shape[1]), jnp.float32)],
        interpret=interpret,
    )(system, rhs)


def partner(array, axis, bit):
    return lax.ppermute(array, axis, [(i, i ^ 1 << bit) for i in range(lax.axis_size(axis))])


def reduce_scatter(partial_value, order, position):
    bits = len(order)
    value = partial_value.reshape((2,) * bits + partial_value.shape[1:])
    remaining = list(range(bits - 1, -1, -1))
    for level in order:
        axis = remaining.index(level)
        own_bit = position // 2**level % 2
        kept = lax.dynamic_index_in_dim(value, own_bit, axis=axis, keepdims=False)
        sent = lax.dynamic_index_in_dim(value, 1 - own_bit, axis=axis, keepdims=False)
        value = kept + partner(sent, "ex", level)
        remaining.remove(level)
    return value


def all_gather(block, order, position):
    value = block
    present = []
    for level in reversed(order):
        received = partner(value, "ex", level)
        high_side = position // 2**level % 2 == 1
        low = jnp.where(high_side, received, value)
        high = jnp.where(high_side, value, received)
        present.append(level)
        present.sort(reverse=True)
        value = jnp.stack([low, high], axis=present.index(level))
    return value.reshape((-1,) + block.shape[1:])


def bit_orders(bits):
    first = list(range(bits))
    if bits < 4:
        return [first]
    rest = list(range(4, bits))
    return [[0, 1, 2, 3] + rest, [0, 2, 1, 3] + rest, [0, 1, 3, 2] + rest, [0, 2, 3, 1] + rest]


def on_device(grads, proj, target_ids, target_counts):
    count_ex = lax.axis_size("ex")
    bits = count_ex.bit_length() - 1
    position = lax.axis_index("ex")
    ex_rows = grads.shape[0]
    examples = ex_rows * count_ex
    sketch_width = proj.shape[1]
    with jax.named_scope("gradient_exchange"):
        columns = lax.all_to_all(grads, "ex", split_axis=1, concat_axis=0, tiled=True)
    with jax.named_scope("partial_projection"):
        partial_value = jnp.dot(columns, proj, preferred_element_type=jnp.float32)
    orders = bit_orders(bits)
    width = sketch_width // len(orders)
    owned, gathered = [], []
    for half, order in enumerate(orders):
        with jax.named_scope("sketch_reduce"):
            part = reduce_scatter(
                partial_value[:, half * width:(half + 1) * width].reshape(
                    count_ex, ex_rows, width
                ),
                order,
                position,
            )
        with jax.named_scope("sketch_gather"):
            gathered.append(all_gather(part, order, position))
        owned.append(part)
    sketch = jnp.concatenate(owned, axis=1)
    sketch_all = jnp.concatenate(gathered, axis=1)
    slot_count = target_ids.shape[1]
    live_slot = jnp.arange(slot_count, dtype=jnp.int32)[None, :] < target_counts[:, None]
    example_index = jnp.arange(examples, dtype=jnp.int32)
    matches = (target_ids[:, :, None] == example_index[None, None, :]) & live_slot[:, :, None]
    weight = jnp.sum(matches.astype(jnp.float32), axis=1) / target_counts[:, None].astype(
        jnp.float32
    )
    if examples < sketch_width and examples % 128 == 0:
        with jax.named_scope("kernel_matrix"):
            kernel = jnp.dot(sketch_all, sketch_all.T, precision=lax.Precision.HIGHEST)
        with jax.named_scope("kernel_solve"):
            system = kernel / jnp.float32(examples) + 0.1 * jnp.eye(examples, dtype=jnp.float32)
            lanes = -(-weight.shape[0] // 128) * 128
            rhs = jnp.pad(weight.T, ((0, 0), (0, lanes - weight.shape[0])))
            coeffs = spd_solve(system, rhs, block=min(128, examples))[:, : weight.shape[0]]
        own_kernel = lax.dynamic_slice_in_dim(kernel, position * ex_rows, ex_rows, axis=0)
        scores = jnp.dot(own_kernel, coeffs, precision=lax.Precision.HIGHEST)
    else:
        with jax.named_scope("gram_solve"):
            gram_matrix = jnp.dot(sketch_all.T, sketch_all, precision=lax.Precision.HIGHEST)
            domain = jnp.dot(weight, sketch_all, precision=lax.Precision.HIGHEST)
            hessian = gram_matrix / jnp.float32(examples) + 0.1 * jnp.eye(
                sketch_width, dtype=jnp.float32
            )
            factor = jnp.linalg.cholesky(hessian)
            middle = lax.linalg.triangular_solve(factor, domain.T, left_side=True, lower=True)
            solved = lax.linalg.triangular_solve(
                factor, middle, left_side=True, lower=True, transpose_a=True
            )
        scores = jnp.dot(sketch, solved, precision=lax.Precision.HIGHEST)
    return (scores, sketch)


def solution(mesh):
    placed = (P(("groups", "ex"), None), P("ex", None), P(), P())
    return jax.shard_map(
        on_device,
        mesh=mesh,
        in_specs=placed,
        out_specs=(P(("groups", "ex"), None), P(("groups", "ex"), None)),
        check_vma=False,
    )
```

```python
import jax
import jax.numpy as jnp
from jax import lax
from jax.sharding import PartitionSpec as P
import functools
from jax.experimental import pallas as pl
from jax.experimental.pallas import tpu as pltpu

HI = lax.Precision.HIGHEST

def _invert_block(block):
    size = block.shape[0]
    lane = lax.broadcasted_iota(jnp.int32, block.shape, 1)
    sub = lax.broadcasted_iota(jnp.int32, block.shape, 0)
    lane_row = lax.broadcasted_iota(jnp.int32, (1, size), 1)
    sub_col = lax.broadcasted_iota(jnp.int32, (size, 1), 0)

    def pick(row, k):
        return jnp.sum(jnp.where(lane_row == k, row, 0.0), axis=1, keepdims=True)

    def pair_pivot(first, second, k):
        p00 = pick(first, k)
        p01 = pick(first, k + 1)
        p10 = pick(second, k)
        p11 = pick(second, k + 1)
        det = p00 * p11 - p01 * p10
        ident0 = jnp.where(lane_row == k, 1.0, jnp.where(lane_row == k + 1, 0.0, first))
        ident1 = jnp.where(lane_row == k, 0.0, jnp.where(lane_row == k + 1, 1.0, second))
        scaled0 = (p11 * ident0 - p01 * ident1) / det
        scaled1 = (p00 * ident1 - p10 * ident0) / det
        return scaled0, scaled1

    def eliminate(row, k, scaled0, scaled1):
        f0 = pick(row, k)
        f1 = pick(row, k + 1)
        kept = jnp.where((lane_row == k) | (lane_row == k + 1), 0.0, row)
        return kept - f0 * scaled0 - f1 * scaled1

    def step(h, a):
        k = 4 * h
        base = k - k % 8
        tile = jnp.sum(
            jnp.where((sub >= base) & (sub < base + 8), a, 0.0).reshape(size // 8, 8, size), axis=0)
        in_tile = lax.broadcasted_iota(jnp.int32, (8, size), 0)
        rows = [jnp.sum(jnp.where(in_tile == k % 8 + t, tile, 0.0), axis=0, keepdims=True)
                for t in range(4)]
        cols = [jnp.sum(jnp.where(lane == k + t, a, 0.0), axis=1, keepdims=True) for t in range(4)]
        s0, s1 = pair_pivot(rows[0], rows[1], k)
        r2 = eliminate(rows[2], k, s0, s1)
        r3 = eliminate(rows[3], k, s0, s1)
        s2, s3 = pair_pivot(r2, r3, k + 2)
        s0 = eliminate(s0, k + 2, s2, s3)
        s1 = eliminate(s1, k + 2, s2, s3)
        slab = (s0, s1, s2, s3)
        pivot_rows = (sub_col >= k) & (sub_col < k + 4)
        a = jnp.where((lane >= k) & (lane < k + 4), 0.0, a)
        for t in range(4):
            a = a - jnp.where(pivot_rows, 0.0, cols[t]) * slab[t]
        for t in range(4):
            a = jnp.where(sub == k + t, slab[t], a)
        return a

    return lax.fori_loop(0, size // 4, step, block)


def _solve_kernel(m_ref, w_ref, y_ref, a_ref, *, block):
    n = m_ref.shape[0]
    a_ref[:, :n] = m_ref[...]
    a_ref[:, n:] = w_ref[...]
    blocks = n // block
    for j in range(blocks):
        lo = j * block
        hi = lo + block
        inverse = _invert_block(a_ref[lo:hi, lo:hi])
        pivot_rows = jnp.dot(inverse, a_ref[lo:hi, hi:], precision=HI,
                             preferred_element_type=jnp.float32)
        for i in range(blocks):
            if i == j:
                continue
            r = i * block
            a_ref[r:r + block, hi:] = a_ref[r:r + block, hi:] - jnp.dot(
                a_ref[r:r + block, lo:hi], pivot_rows, precision=HI,
                preferred_element_type=jnp.float32)
        a_ref[lo:hi, hi:] = pivot_rows
    y_ref[...] = a_ref[:, n:]


def spd_solve(system, rhs, block=128, interpret=False):
    n = system.shape[0]
    return pl.pallas_call(
        functools.partial(_solve_kernel, block=block),
        out_shape=jax.ShapeDtypeStruct(rhs.shape, jnp.float32),
        scratch_shapes=[pltpu.VMEM((n, n + rhs.shape[1]), jnp.float32)],
        interpret=interpret,
    )(system, rhs)


def partner(array, axis, bit):
    return lax.ppermute(array, axis, [(i, i ^ 1 << bit) for i in range(lax.axis_size(axis))])


def reduce_and_gather(partial_value, order, position):
    bits = len(order)
    rows = partial_value.shape[1:]
    value = partial_value.reshape((2,) * bits + rows)
    remaining = list(range(bits - 1, -1, -1))
    for level in order[:-1]:
        axis = remaining.index(level)
        own_bit = position // 2**level % 2
        kept = lax.dynamic_index_in_dim(value, own_bit, axis=axis, keepdims=False)
        sent = lax.dynamic_index_in_dim(value, 1 - own_bit, axis=axis, keepdims=False)
        value = kept + partner(sent, "ex", level)
        remaining.remove(level)
    last = order[-1]
    value = value + partner(value, "ex", last)
    own = lax.dynamic_index_in_dim(value, position // 2**last % 2, axis=0, keepdims=False)
    present = [last]
    for level in reversed(order[:-1]):
        received = partner(value, "ex", level)
        high_side = position // 2**level % 2 == 1
        low = jnp.where(high_side, received, value)
        high = jnp.where(high_side, value, received)
        present.append(level)
        present.sort(reverse=True)
        value = jnp.stack([low, high], axis=present.index(level))
    return own, value.reshape((-1,) + rows[1:])


def bit_orders(bits):
    first = list(range(bits))
    if bits < 4:
        return [first]
    rest = list(range(4, bits))
    return [[0, 1, 2, 3] + rest, [0, 2, 1, 3] + rest, [0, 1, 3, 2] + rest, [0, 2, 3, 1] + rest]


def on_device(grads, proj, target_ids, target_counts):
    count_ex = lax.axis_size("ex")
    bits = count_ex.bit_length() - 1
    position = lax.axis_index("ex")
    ex_rows = grads.shape[0]
    examples = ex_rows * count_ex
    sketch_width = proj.shape[1]
    with jax.named_scope("gradient_exchange"):
        columns = lax.all_to_all(grads, "ex", split_axis=1, concat_axis=0, tiled=True)
    with jax.named_scope("partial_projection"):
        partial_value = jnp.dot(columns, proj, preferred_element_type=jnp.float32)
    orders = bit_orders(bits)
    width = sketch_width // len(orders)
    owned, gathered = [], []
    for half, order in enumerate(orders):
        with jax.named_scope("sketch_reduce_gather"):
            part, every = reduce_and_gather(
                partial_value[:, half * width:(half + 1) * width].reshape(
                    count_ex, ex_rows, width
                ),
                order,
                position,
            )
        gathered.append(every)
        owned.append(part)
    sketch = jnp.concatenate(owned, axis=1)
    sketch_all = jnp.concatenate(gathered, axis=1)
    slot_count = target_ids.shape[1]
    live_slot = jnp.arange(slot_count, dtype=jnp.int32)[None, :] < target_counts[:, None]
    example_index = jnp.arange(examples, dtype=jnp.int32)
    matches = (target_ids[:, :, None] == example_index[None, None, :]) & live_slot[:, :, None]
    weight = jnp.sum(matches.astype(jnp.float32), axis=1) / target_counts[:, None].astype(
        jnp.float32
    )
    if examples < sketch_width and examples % 128 == 0:
        with jax.named_scope("kernel_matrix"):
            kernel = jnp.dot(sketch_all, sketch_all.T, precision=lax.Precision.HIGHEST)
        with jax.named_scope("kernel_solve"):
            system = kernel / jnp.float32(examples) + 0.1 * jnp.eye(examples, dtype=jnp.float32)
            lanes = -(-weight.shape[0] // 128) * 128
            rhs = jnp.pad(weight.T, ((0, 0), (0, lanes - weight.shape[0])))
            coeffs = spd_solve(system, rhs, block=min(128, examples))[:, : weight.shape[0]]
        own_kernel = lax.dynamic_slice_in_dim(kernel, position * ex_rows, ex_rows, axis=0)
        scores = jnp.dot(own_kernel, coeffs, precision=lax.Precision.HIGHEST)
    else:
        with jax.named_scope("gram_solve"):
            gram_matrix = jnp.dot(sketch_all.T, sketch_all, precision=lax.Precision.HIGHEST)
            domain = jnp.dot(weight, sketch_all, precision=lax.Precision.HIGHEST)
            hessian = gram_matrix / jnp.float32(examples) + 0.1 * jnp.eye(
                sketch_width, dtype=jnp.float32
            )
            factor = jnp.linalg.cholesky(hessian)
            middle = lax.linalg.triangular_solve(factor, domain.T, left_side=True, lower=True)
            solved = lax.linalg.triangular_solve(
                factor, middle, left_side=True, lower=True, transpose_a=True
            )
        scores = jnp.dot(sketch, solved, precision=lax.Precision.HIGHEST)
    return (scores, sketch)


def solution(mesh):
    placed = (P(("groups", "ex"), None), P("ex", None), P(), P())
    return jax.shard_map(
        on_device,
        mesh=mesh,
        in_specs=placed,
        out_specs=(P(("groups", "ex"), None), P(("groups", "ex"), None)),
        check_vma=False,
    )
```

```python
import jax
import jax.numpy as jnp
from jax import lax
from jax.sharding import PartitionSpec as P
import functools
from jax.experimental import pallas as pl
from jax.experimental.pallas import tpu as pltpu

HI = lax.Precision.HIGHEST

def _invert_block(block):
    size = block.shape[0]
    lane = lax.broadcasted_iota(jnp.int32, block.shape, 1)
    sub = lax.broadcasted_iota(jnp.int32, block.shape, 0)
    lane_row = lax.broadcasted_iota(jnp.int32, (1, size), 1)
    sub_col = lax.broadcasted_iota(jnp.int32, (size, 1), 0)

    def pick(row, k):
        return jnp.sum(jnp.where(lane_row == k, row, 0.0), axis=1, keepdims=True)

    def pair_pivot(first, second, k):
        p00 = pick(first, k)
        p01 = pick(first, k + 1)
        p10 = pick(second, k)
        p11 = pick(second, k + 1)
        det = p00 * p11 - p01 * p10
        ident0 = jnp.where(lane_row == k, 1.0, jnp.where(lane_row == k + 1, 0.0, first))
        ident1 = jnp.where(lane_row == k, 0.0, jnp.where(lane_row == k + 1, 1.0, second))
        scaled0 = (p11 * ident0 - p01 * ident1) / det
        scaled1 = (p00 * ident1 - p10 * ident0) / det
        return scaled0, scaled1

    def eliminate(row, k, scaled0, scaled1):
        f0 = pick(row, k)
        f1 = pick(row, k + 1)
        kept = jnp.where((lane_row == k) | (lane_row == k + 1), 0.0, row)
        return kept - f0 * scaled0 - f1 * scaled1

    in_tile = lax.broadcasted_iota(jnp.int32, (8, size), 0)
    tile_lane = lax.broadcasted_iota(jnp.int32, (8, size), 1)

    def step(h, a):
        k = 8 * h
        in_rows = (sub >= k) & (sub < k + 8)
        tile = jnp.sum(jnp.where(in_rows, a, 0.0).reshape(size // 8, 8, size), axis=0)
        cols = [jnp.sum(jnp.where(lane == k + t, a, 0.0), axis=1, keepdims=True) for t in range(8)]
        for u in range(4):
            p = k + 2 * u
            first = jnp.sum(jnp.where(in_tile == 2 * u, tile, 0.0), axis=0, keepdims=True)
            second = jnp.sum(jnp.where(in_tile == 2 * u + 1, tile, 0.0), axis=0, keepdims=True)
            s_first, s_second = pair_pivot(first, second, p)
            f0 = jnp.sum(jnp.where(tile_lane == p, tile, 0.0), axis=1, keepdims=True)
            f1 = jnp.sum(jnp.where(tile_lane == p + 1, tile, 0.0), axis=1, keepdims=True)
            tile = jnp.where((tile_lane == p) | (tile_lane == p + 1), 0.0, tile) - f0 * s_first - f1 * s_second
            tile = jnp.where(in_tile == 2 * u, s_first, jnp.where(in_tile == 2 * u + 1, s_second, tile))
        slab = [jnp.sum(jnp.where(in_tile == t, tile, 0.0), axis=0, keepdims=True) for t in range(8)]
        a = jnp.where((lane >= k) & (lane < k + 8), 0.0, a)
        for t in range(8):
            a = a - jnp.where(in_rows, 0.0, cols[t]) * slab[t]
        return jnp.where(in_rows, jnp.tile(tile, (size // 8, 1)), a)

    return lax.fori_loop(0, size // 8, step, block)


def _solve_kernel(m_ref, w_ref, y_ref, a_ref, *, block):
    n = m_ref.shape[0]
    a_ref[:, :n] = m_ref[...]
    a_ref[:, n:] = w_ref[...]
    blocks = n // block
    for j in range(blocks):
        lo = j * block
        hi = lo + block
        inverse = _invert_block(a_ref[lo:hi, lo:hi])
        pivot_rows = jnp.dot(inverse, a_ref[lo:hi, hi:], precision=HI,
                             preferred_element_type=jnp.float32)
        for i in range(blocks):
            if i == j:
                continue
            r = i * block
            a_ref[r:r + block, hi:] = a_ref[r:r + block, hi:] - jnp.dot(
                a_ref[r:r + block, lo:hi], pivot_rows, precision=HI,
                preferred_element_type=jnp.float32)
        a_ref[lo:hi, hi:] = pivot_rows
    y_ref[...] = a_ref[:, n:]


def spd_solve(system, rhs, block=128, interpret=False):
    n = system.shape[0]
    return pl.pallas_call(
        functools.partial(_solve_kernel, block=block),
        out_shape=jax.ShapeDtypeStruct(rhs.shape, jnp.float32),
        scratch_shapes=[pltpu.VMEM((n, n + rhs.shape[1]), jnp.float32)],
        interpret=interpret,
    )(system, rhs)


def partner(array, axis, bit):
    return lax.ppermute(array, axis, [(i, i ^ 1 << bit) for i in range(lax.axis_size(axis))])


def reduce_and_gather(partial_value, order, position):
    bits = len(order)
    rows = partial_value.shape[1:]
    value = partial_value.reshape((2,) * bits + rows)
    remaining = list(range(bits - 1, -1, -1))
    for level in order[:-1]:
        axis = remaining.index(level)
        own_bit = position // 2**level % 2
        kept = lax.dynamic_index_in_dim(value, own_bit, axis=axis, keepdims=False)
        sent = lax.dynamic_index_in_dim(value, 1 - own_bit, axis=axis, keepdims=False)
        value = kept + partner(sent, "ex", level)
        remaining.remove(level)
    last = order[-1]
    value = value + partner(value, "ex", last)
    own = lax.dynamic_index_in_dim(value, position // 2**last % 2, axis=0, keepdims=False)
    present = [last]
    for level in reversed(order[:-1]):
        received = partner(value, "ex", level)
        high_side = position // 2**level % 2 == 1
        low = jnp.where(high_side, received, value)
        high = jnp.where(high_side, value, received)
        present.append(level)
        present.sort(reverse=True)
        value = jnp.stack([low, high], axis=present.index(level))
    return own, value.reshape((-1,) + rows[1:])


def bit_orders(bits):
    first = list(range(bits))
    if bits < 4:
        return [first]
    rest = list(range(4, bits))
    return [[0, 1, 2, 3] + rest, [0, 2, 1, 3] + rest, [0, 1, 3, 2] + rest, [0, 2, 3, 1] + rest]


def on_device(grads, proj, target_ids, target_counts):
    count_ex = lax.axis_size("ex")
    bits = count_ex.bit_length() - 1
    position = lax.axis_index("ex")
    ex_rows = grads.shape[0]
    examples = ex_rows * count_ex
    sketch_width = proj.shape[1]
    with jax.named_scope("gradient_exchange"):
        columns = lax.all_to_all(grads, "ex", split_axis=1, concat_axis=0, tiled=True)
    with jax.named_scope("partial_projection"):
        partial_value = jnp.dot(columns, proj, preferred_element_type=jnp.float32)
    orders = bit_orders(bits)
    width = sketch_width // len(orders)
    owned, gathered = [], []
    for half, order in enumerate(orders):
        with jax.named_scope("sketch_reduce_gather"):
            part, every = reduce_and_gather(
                partial_value[:, half * width:(half + 1) * width].reshape(
                    count_ex, ex_rows, width
                ),
                order,
                position,
            )
        gathered.append(every)
        owned.append(part)
    sketch = jnp.concatenate(owned, axis=1)
    sketch_all = jnp.concatenate(gathered, axis=1)
    slot_count = target_ids.shape[1]
    live_slot = jnp.arange(slot_count, dtype=jnp.int32)[None, :] < target_counts[:, None]
    example_index = jnp.arange(examples, dtype=jnp.int32)
    matches = (target_ids[:, :, None] == example_index[None, None, :]) & live_slot[:, :, None]
    weight = jnp.sum(matches.astype(jnp.float32), axis=1) / target_counts[:, None].astype(
        jnp.float32
    )
    if examples < sketch_width and examples % 128 == 0:
        with jax.named_scope("kernel_matrix"):
            kernel = jnp.dot(sketch_all, sketch_all.T, precision=lax.Precision.HIGHEST)
        with jax.named_scope("kernel_solve"):
            system = kernel / jnp.float32(examples) + 0.1 * jnp.eye(examples, dtype=jnp.float32)
            lanes = -(-weight.shape[0] // 128) * 128
            rhs = jnp.pad(weight.T, ((0, 0), (0, lanes - weight.shape[0])))
            coeffs = spd_solve(system, rhs, block=min(128, examples))[:, : weight.shape[0]]
        own_kernel = lax.dynamic_slice_in_dim(kernel, position * ex_rows, ex_rows, axis=0)
        scores = jnp.dot(own_kernel, coeffs, precision=lax.Precision.HIGHEST)
    else:
        with jax.named_scope("gram_solve"):
            gram_matrix = jnp.dot(sketch_all.T, sketch_all, precision=lax.Precision.HIGHEST)
            domain = jnp.dot(weight, sketch_all, precision=lax.Precision.HIGHEST)
            hessian = gram_matrix / jnp.float32(examples) + 0.1 * jnp.eye(
                sketch_width, dtype=jnp.float32
            )
            factor = jnp.linalg.cholesky(hessian)
            middle = lax.linalg.triangular_solve(factor, domain.T, left_side=True, lower=True)
            solved = lax.linalg.triangular_solve(
                factor, middle, left_side=True, lower=True, transpose_a=True
            )
        scores = jnp.dot(sketch, solved, precision=lax.Precision.HIGHEST)
    return (scores, sketch)


def solution(mesh):
    placed = (P(("groups", "ex"), None), P("ex", None), P(), P())
    return jax.shard_map(
        on_device,
        mesh=mesh,
        in_specs=placed,
        out_specs=(P(("groups", "ex"), None), P(("groups", "ex"), None)),
        check_vma=False,
    )
```

```python
import jax
import jax.numpy as jnp
from jax import lax
from jax.sharding import PartitionSpec as P
import functools
from jax.experimental import pallas as pl
from jax.experimental.pallas import tpu as pltpu

HI = lax.Precision.HIGHEST

def _invert_block(block):
    size = block.shape[0]
    lane = lax.broadcasted_iota(jnp.int32, block.shape, 1)
    sub = lax.broadcasted_iota(jnp.int32, block.shape, 0)
    lane_row = lax.broadcasted_iota(jnp.int32, (1, size), 1)
    sub_col = lax.broadcasted_iota(jnp.int32, (size, 1), 0)

    def pick(row, k):
        return jnp.sum(jnp.where(lane_row == k, row, 0.0), axis=1, keepdims=True)

    def pair_pivot(first, second, k):
        p00 = pick(first, k)
        p01 = pick(first, k + 1)
        p10 = pick(second, k)
        p11 = pick(second, k + 1)
        det = p00 * p11 - p01 * p10
        ident0 = jnp.where(lane_row == k, 1.0, jnp.where(lane_row == k + 1, 0.0, first))
        ident1 = jnp.where(lane_row == k, 0.0, jnp.where(lane_row == k + 1, 1.0, second))
        scaled0 = (p11 * ident0 - p01 * ident1) / det
        scaled1 = (p00 * ident1 - p10 * ident0) / det
        return scaled0, scaled1

    def eliminate(row, k, scaled0, scaled1):
        f0 = pick(row, k)
        f1 = pick(row, k + 1)
        kept = jnp.where((lane_row == k) | (lane_row == k + 1), 0.0, row)
        return kept - f0 * scaled0 - f1 * scaled1

    in_tile = lax.broadcasted_iota(jnp.int32, (8, size), 0)
    tile_lane = lax.broadcasted_iota(jnp.int32, (8, size), 1)

    def step(h, a):
        k = 8 * h
        in_rows = (sub >= k) & (sub < k + 8)
        tile = jnp.sum(jnp.where(in_rows, a, 0.0).reshape(size // 8, 8, size), axis=0)
        cols = [jnp.sum(jnp.where(lane == k + t, a, 0.0), axis=1, keepdims=True) for t in range(8)]
        for u in range(4):
            p = k + 2 * u
            first = jnp.sum(jnp.where(in_tile == 2 * u, tile, 0.0), axis=0, keepdims=True)
            second = jnp.sum(jnp.where(in_tile == 2 * u + 1, tile, 0.0), axis=0, keepdims=True)
            s_first, s_second = pair_pivot(first, second, p)
            f0 = jnp.sum(jnp.where(tile_lane == p, tile, 0.0), axis=1, keepdims=True)
            f1 = jnp.sum(jnp.where(tile_lane == p + 1, tile, 0.0), axis=1, keepdims=True)
            tile = jnp.where((tile_lane == p) | (tile_lane == p + 1), 0.0, tile) - f0 * s_first - f1 * s_second
            tile = jnp.where(in_tile == 2 * u, s_first, jnp.where(in_tile == 2 * u + 1, s_second, tile))
        slab = [jnp.sum(jnp.where(in_tile == t, tile, 0.0), axis=0, keepdims=True) for t in range(8)]
        a = jnp.where((lane >= k) & (lane < k + 8), 0.0, a)
        for t in range(8):
            a = a - jnp.where(in_rows, 0.0, cols[t]) * slab[t]
        return jnp.where(in_rows, jnp.tile(tile, (size // 8, 1)), a)

    return lax.fori_loop(0, size // 8, step, block)


def _solve_kernel(m_ref, w_ref, y_ref, a_ref, *, block):
    n = m_ref.shape[0]
    a_ref[:, :n] = m_ref[...]
    a_ref[:, n:] = w_ref[...]
    blocks = n // block
    for j in range(blocks):
        lo = j * block
        hi = lo + block
        inverse = _invert_block(a_ref[lo:hi, lo:hi])
        pivot_rows = jnp.dot(inverse, a_ref[lo:hi, hi:], precision=HI,
                             preferred_element_type=jnp.float32)
        for i in range(blocks):
            if i == j:
                continue
            r = i * block
            a_ref[r:r + block, hi:] = a_ref[r:r + block, hi:] - jnp.dot(
                a_ref[r:r + block, lo:hi], pivot_rows, precision=HI,
                preferred_element_type=jnp.float32)
        a_ref[lo:hi, hi:] = pivot_rows
    y_ref[...] = a_ref[:, n:]


def spd_solve(system, rhs, block=128, interpret=False):
    n = system.shape[0]
    return pl.pallas_call(
        functools.partial(_solve_kernel, block=block),
        out_shape=jax.ShapeDtypeStruct(rhs.shape, jnp.float32),
        scratch_shapes=[pltpu.VMEM((n, n + rhs.shape[1]), jnp.float32)],
        interpret=interpret,
    )(system, rhs)


def partner(array, axis, bit):
    return lax.ppermute(array, axis, [(i, i ^ 1 << bit) for i in range(lax.axis_size(axis))])


def reduce_and_gather(first_kept, first_sent, order, position):
    bits = len(order)
    rows = first_kept.shape[1:]
    value = first_kept.reshape((2,) * (bits - 1) + rows) + partner(
        first_sent.reshape((2,) * (bits - 1) + rows), "ex", order[0])
    remaining = [level for level in range(bits - 1, -1, -1) if level != order[0]]
    for level in order[1:-1]:
        axis = remaining.index(level)
        own_bit = position // 2**level % 2
        kept = lax.dynamic_index_in_dim(value, own_bit, axis=axis, keepdims=False)
        sent = lax.dynamic_index_in_dim(value, 1 - own_bit, axis=axis, keepdims=False)
        value = kept + partner(sent, "ex", level)
        remaining.remove(level)
    last = order[-1]
    value = value + partner(value, "ex", last)
    own = lax.dynamic_index_in_dim(value, position // 2**last % 2, axis=0, keepdims=False)
    present = [last]
    for level in reversed(order[:-1]):
        received = partner(value, "ex", level)
        high_side = position // 2**level % 2 == 1
        low = jnp.where(high_side, received, value)
        high = jnp.where(high_side, value, received)
        present.append(level)
        present.sort(reverse=True)
        value = jnp.stack([low, high], axis=present.index(level))
    return own, value.reshape((-1,) + rows[1:])


def bit_orders(bits):
    first = list(range(bits))
    if bits < 4:
        return [first]
    rest = list(range(4, bits))
    return [[0, 1, 2, 3] + rest, [0, 2, 1, 3] + rest, [0, 1, 3, 2] + rest, [0, 2, 3, 1] + rest]


def on_device(grads, proj, target_ids, target_counts):
    count_ex = lax.axis_size("ex")
    bits = count_ex.bit_length() - 1
    position = lax.axis_index("ex")
    ex_rows = grads.shape[0]
    examples = ex_rows * count_ex
    sketch_width = proj.shape[1]
    with jax.named_scope("gradient_exchange"):
        columns = lax.all_to_all(grads, "ex", split_axis=1, concat_axis=0, tiled=True)
    by_low_bit = columns.reshape(count_ex // 2, 2, ex_rows, columns.shape[1])
    own_low = position % 2
    with jax.named_scope("partial_projection"):
        sent_value = jnp.dot(
            lax.dynamic_index_in_dim(by_low_bit, 1 - own_low, axis=1, keepdims=False), proj,
            preferred_element_type=jnp.float32,
        )
        kept_value = jnp.dot(
            lax.dynamic_index_in_dim(by_low_bit, own_low, axis=1, keepdims=False), proj,
            preferred_element_type=jnp.float32,
        )
    orders = bit_orders(bits)
    width = sketch_width // len(orders)
    owned, gathered = [], []
    for half, order in enumerate(orders):
        with jax.named_scope("sketch_reduce_gather"):
            part, every = reduce_and_gather(
                kept_value[..., half * width:(half + 1) * width],
                sent_value[..., half * width:(half + 1) * width],
                order,
                position,
            )
        gathered.append(every)
        owned.append(part)
    sketch = jnp.concatenate(owned, axis=1)
    sketch_all = jnp.concatenate(gathered, axis=1)
    slot_count = target_ids.shape[1]
    live_slot = jnp.arange(slot_count, dtype=jnp.int32)[None, :] < target_counts[:, None]
    example_index = jnp.arange(examples, dtype=jnp.int32)
    matches = (target_ids[:, :, None] == example_index[None, None, :]) & live_slot[:, :, None]
    weight = jnp.sum(matches.astype(jnp.float32), axis=1) / target_counts[:, None].astype(
        jnp.float32
    )
    if examples < sketch_width and examples % 128 == 0:
        with jax.named_scope("kernel_matrix"):
            kernel = jnp.dot(sketch_all, sketch_all.T, precision=lax.Precision.HIGHEST)
        with jax.named_scope("kernel_solve"):
            system = kernel / jnp.float32(examples) + 0.1 * jnp.eye(examples, dtype=jnp.float32)
            lanes = -(-weight.shape[0] // 128) * 128
            rhs = jnp.pad(weight.T, ((0, 0), (0, lanes - weight.shape[0])))
            coeffs = spd_solve(system, rhs, block=min(128, examples))[:, : weight.shape[0]]
        own_kernel = lax.dynamic_slice_in_dim(kernel, position * ex_rows, ex_rows, axis=0)
        scores = jnp.dot(own_kernel, coeffs, precision=lax.Precision.HIGHEST)
    else:
        with jax.named_scope("gram_solve"):
            gram_matrix = jnp.dot(sketch_all.T, sketch_all, precision=lax.Precision.HIGHEST)
            domain = jnp.dot(weight, sketch_all, precision=lax.Precision.HIGHEST)
            hessian = gram_matrix / jnp.float32(examples) + 0.1 * jnp.eye(
                sketch_width, dtype=jnp.float32
            )
            factor = jnp.linalg.cholesky(hessian)
            middle = lax.linalg.triangular_solve(factor, domain.T, left_side=True, lower=True)
            solved = lax.linalg.triangular_solve(
                factor, middle, left_side=True, lower=True, transpose_a=True
            )
        scores = jnp.dot(sketch, solved, precision=lax.Precision.HIGHEST)
    return (scores, sketch)


def solution(mesh):
    placed = (P(("groups", "ex"), None), P("ex", None), P(), P())
    return jax.shard_map(
        on_device,
        mesh=mesh,
        in_specs=placed,
        out_specs=(P(("groups", "ex"), None), P(("groups", "ex"), None)),
        check_vma=False,
    )
```

```python
import jax
import jax.numpy as jnp
from jax import lax
from jax.sharding import PartitionSpec as P
import functools
from jax.experimental import pallas as pl
from jax.experimental.pallas import tpu as pltpu

HI = lax.Precision.HIGHEST

def _invert_block(block):
    size = block.shape[0]
    lane = lax.broadcasted_iota(jnp.int32, block.shape, 1)
    sub = lax.broadcasted_iota(jnp.int32, block.shape, 0)
    lane_row = lax.broadcasted_iota(jnp.int32, (1, size), 1)
    sub_col = lax.broadcasted_iota(jnp.int32, (size, 1), 0)

    def pick(row, k):
        return jnp.sum(jnp.where(lane_row == k, row, 0.0), axis=1, keepdims=True)

    def pair_pivot(first, second, k):
        p00 = pick(first, k)
        p01 = pick(first, k + 1)
        p10 = pick(second, k)
        p11 = pick(second, k + 1)
        det = p00 * p11 - p01 * p10
        ident0 = jnp.where(lane_row == k, 1.0, jnp.where(lane_row == k + 1, 0.0, first))
        ident1 = jnp.where(lane_row == k, 0.0, jnp.where(lane_row == k + 1, 1.0, second))
        scaled0 = (p11 * ident0 - p01 * ident1) / det
        scaled1 = (p00 * ident1 - p10 * ident0) / det
        return scaled0, scaled1

    def eliminate(row, k, scaled0, scaled1):
        f0 = pick(row, k)
        f1 = pick(row, k + 1)
        kept = jnp.where((lane_row == k) | (lane_row == k + 1), 0.0, row)
        return kept - f0 * scaled0 - f1 * scaled1

    in_tile = lax.broadcasted_iota(jnp.int32, (8, size), 0)
    tile_lane = lax.broadcasted_iota(jnp.int32, (8, size), 1)

    def step(h, a):
        k = 8 * h
        in_rows = (sub >= k) & (sub < k + 8)
        tile = jnp.sum(jnp.where(in_rows, a, 0.0).reshape(size // 8, 8, size), axis=0)
        cols = [jnp.sum(jnp.where(lane == k + t, a, 0.0), axis=1, keepdims=True) for t in range(8)]
        for u in range(4):
            p = k + 2 * u
            first = jnp.sum(jnp.where(in_tile == 2 * u, tile, 0.0), axis=0, keepdims=True)
            second = jnp.sum(jnp.where(in_tile == 2 * u + 1, tile, 0.0), axis=0, keepdims=True)
            s_first, s_second = pair_pivot(first, second, p)
            f0 = jnp.sum(jnp.where(tile_lane == p, tile, 0.0), axis=1, keepdims=True)
            f1 = jnp.sum(jnp.where(tile_lane == p + 1, tile, 0.0), axis=1, keepdims=True)
            tile = jnp.where((tile_lane == p) | (tile_lane == p + 1), 0.0, tile) - f0 * s_first - f1 * s_second
            tile = jnp.where(in_tile == 2 * u, s_first, jnp.where(in_tile == 2 * u + 1, s_second, tile))
        slab = [jnp.sum(jnp.where(in_tile == t, tile, 0.0), axis=0, keepdims=True) for t in range(8)]
        a = jnp.where((lane >= k) & (lane < k + 8), 0.0, a)
        for t in range(8):
            a = a - jnp.where(in_rows, 0.0, cols[t]) * slab[t]
        return jnp.where(in_rows, jnp.tile(tile, (size // 8, 1)), a)

    return lax.fori_loop(0, size // 8, step, block)


def _solve_kernel(m_ref, w_ref, y_ref, a_ref, *, block):
    n = m_ref.shape[0]
    a_ref[:, :n] = m_ref[...]
    a_ref[:, n:] = w_ref[...]
    blocks = n // block
    for j in range(blocks):
        lo = j * block
        hi = lo + block
        inverse = _invert_block(a_ref[lo:hi, lo:hi])
        pivot_rows = jnp.dot(inverse, a_ref[lo:hi, hi:], precision=HI,
                             preferred_element_type=jnp.float32)
        for i in range(blocks):
            if i == j:
                continue
            r = i * block
            a_ref[r:r + block, hi:] = a_ref[r:r + block, hi:] - jnp.dot(
                a_ref[r:r + block, lo:hi], pivot_rows, precision=HI,
                preferred_element_type=jnp.float32)
        a_ref[lo:hi, hi:] = pivot_rows
    y_ref[...] = a_ref[:, n:]


def spd_solve(system, rhs, block=128, interpret=False):
    n = system.shape[0]
    return pl.pallas_call(
        functools.partial(_solve_kernel, block=block),
        out_shape=jax.ShapeDtypeStruct(rhs.shape, jnp.float32),
        scratch_shapes=[pltpu.VMEM((n, n + rhs.shape[1]), jnp.float32)],
        interpret=interpret,
    )(system, rhs)


def partner(array, axis, bit):
    return lax.ppermute(array, axis, [(i, i ^ 1 << bit) for i in range(lax.axis_size(axis))])


def reduce_and_gather(partial_value, order, position):
    bits = len(order)
    rows = partial_value.shape[1:]
    value = partial_value.reshape((2,) * bits + rows)
    remaining = list(range(bits - 1, -1, -1))
    for level in order[:-1]:
        axis = remaining.index(level)
        own_bit = position // 2**level % 2
        kept = lax.dynamic_index_in_dim(value, own_bit, axis=axis, keepdims=False)
        sent = lax.dynamic_index_in_dim(value, 1 - own_bit, axis=axis, keepdims=False)
        value = kept + partner(sent, "ex", level)
        remaining.remove(level)
    last = order[-1]
    value = value + partner(value, "ex", last)
    own = lax.dynamic_index_in_dim(value, position // 2**last % 2, axis=0, keepdims=False)
    present = [last]
    for level in reversed(order[:-1]):
        received = partner(value, "ex", level)
        high_side = position // 2**level % 2 == 1
        low = jnp.where(high_side, received, value)
        high = jnp.where(high_side, value, received)
        present.append(level)
        present.sort(reverse=True)
        value = jnp.stack([low, high], axis=present.index(level))
    return own, value.reshape((-1,) + rows[1:])


def bit_orders(bits):
    first = list(range(bits))
    if bits < 4:
        return [first]
    rest = list(range(4, bits))
    return [[0, 1, 2, 3] + rest, [0, 2, 1, 3] + rest, [0, 1, 3, 2] + rest, [0, 2, 3, 1] + rest]


def on_device(grads, proj, target_ids, target_counts):
    count_ex = lax.axis_size("ex")
    bits = count_ex.bit_length() - 1
    position = lax.axis_index("ex")
    ex_rows = grads.shape[0]
    examples = ex_rows * count_ex
    sketch_width = proj.shape[1]
    with jax.named_scope("gradient_exchange"):
        columns = lax.all_to_all(grads, "ex", split_axis=1, concat_axis=0, tiled=True)
    with jax.named_scope("partial_projection"):
        partial_value = jnp.dot(columns, proj, preferred_element_type=jnp.float32)
    orders = bit_orders(bits)
    width = sketch_width // len(orders)
    owned, gathered = [], []
    for half, order in enumerate(orders):
        with jax.named_scope("sketch_reduce_gather"):
            part, every = reduce_and_gather(
                partial_value[:, half * width:(half + 1) * width].reshape(
                    count_ex, ex_rows, width
                ),
                order,
                position,
            )
        gathered.append(every)
        owned.append(part)
    sketch = jnp.concatenate(owned, axis=1)
    sketch_all = jnp.concatenate(gathered, axis=1)
    slot_count = target_ids.shape[1]
    live_slot = jnp.arange(slot_count, dtype=jnp.int32)[None, :] < target_counts[:, None]
    example_index = jnp.arange(examples, dtype=jnp.int32)
    matches = (target_ids[:, :, None] == example_index[None, None, :]) & live_slot[:, :, None]
    weight = jnp.sum(matches.astype(jnp.float32), axis=1) / target_counts[:, None].astype(
        jnp.float32
    )
    if examples < sketch_width and examples % 128 == 0:
        with jax.named_scope("kernel_matrix"):
            kernel = jnp.dot(sketch_all, sketch_all.T, precision=lax.Precision.HIGHEST)
        with jax.named_scope("kernel_solve"):
            system = kernel / jnp.float32(examples) + 0.1 * jnp.eye(examples, dtype=jnp.float32)
            lanes = -(-weight.shape[0] // 128) * 128
            rhs = jnp.pad(weight.T, ((0, 0), (0, lanes - weight.shape[0])))
            coeffs = spd_solve(system, rhs, block=min(128, examples))[:, : weight.shape[0]]
        own_weight = lax.dynamic_slice_in_dim(weight.T, position * ex_rows, ex_rows, axis=0)
        own_coeffs = lax.dynamic_slice_in_dim(coeffs, position * ex_rows, ex_rows, axis=0)
        scores = jnp.float32(examples) * (own_weight - 0.1 * own_coeffs)
    else:
        with jax.named_scope("gram_solve"):
            gram_matrix = jnp.dot(sketch_all.T, sketch_all, precision=lax.Precision.HIGHEST)
            domain = jnp.dot(weight, sketch_all, precision=lax.Precision.HIGHEST)
            hessian = gram_matrix / jnp.float32(examples) + 0.1 * jnp.eye(
                sketch_width, dtype=jnp.float32
            )
            factor = jnp.linalg.cholesky(hessian)
            middle = lax.linalg.triangular_solve(factor, domain.T, left_side=True, lower=True)
            solved = lax.linalg.triangular_solve(
                factor, middle, left_side=True, lower=True, transpose_a=True
            )
        scores = jnp.dot(sketch, solved, precision=lax.Precision.HIGHEST)
    return (scores, sketch)


def solution(mesh):
    placed = (P(("groups", "ex"), None), P("ex", None), P(), P())
    return jax.shard_map(
        on_device,
        mesh=mesh,
        in_specs=placed,
        out_specs=(P(("groups", "ex"), None), P(("groups", "ex"), None)),
        check_vma=False,
    )
```

```python
import jax
import jax.numpy as jnp
from jax import lax
from jax.sharding import PartitionSpec as P
import functools
from jax.experimental import pallas as pl
from jax.experimental.pallas import tpu as pltpu

HI = lax.Precision.HIGHEST

def _invert_block(block):
    size = block.shape[0]
    lane = lax.broadcasted_iota(jnp.int32, block.shape, 1)
    sub = lax.broadcasted_iota(jnp.int32, block.shape, 0)
    lane_row = lax.broadcasted_iota(jnp.int32, (1, size), 1)
    sub_col = lax.broadcasted_iota(jnp.int32, (size, 1), 0)

    def pick(row, k):
        return jnp.sum(jnp.where(lane_row == k, row, 0.0), axis=1, keepdims=True)

    def pair_pivot(first, second, k):
        p00 = pick(first, k)
        p01 = pick(first, k + 1)
        p10 = pick(second, k)
        p11 = pick(second, k + 1)
        det = p00 * p11 - p01 * p10
        ident0 = jnp.where(lane_row == k, 1.0, jnp.where(lane_row == k + 1, 0.0, first))
        ident1 = jnp.where(lane_row == k, 0.0, jnp.where(lane_row == k + 1, 1.0, second))
        scaled0 = (p11 * ident0 - p01 * ident1) / det
        scaled1 = (p00 * ident1 - p10 * ident0) / det
        return scaled0, scaled1

    def eliminate(row, k, scaled0, scaled1):
        f0 = pick(row, k)
        f1 = pick(row, k + 1)
        kept = jnp.where((lane_row == k) | (lane_row == k + 1), 0.0, row)
        return kept - f0 * scaled0 - f1 * scaled1

    in_tile = lax.broadcasted_iota(jnp.int32, (8, size), 0)
    tile_lane = lax.broadcasted_iota(jnp.int32, (8, size), 1)

    def step(h, a):
        k = 8 * h
        in_rows = (sub >= k) & (sub < k + 8)
        tile = jnp.sum(jnp.where(in_rows, a, 0.0).reshape(size // 8, 8, size), axis=0)
        cols = [jnp.sum(jnp.where(lane == k + t, a, 0.0), axis=1, keepdims=True) for t in range(8)]
        for u in range(4):
            p = k + 2 * u
            first = jnp.sum(jnp.where(in_tile == 2 * u, tile, 0.0), axis=0, keepdims=True)
            second = jnp.sum(jnp.where(in_tile == 2 * u + 1, tile, 0.0), axis=0, keepdims=True)
            s_first, s_second = pair_pivot(first, second, p)
            f0 = jnp.sum(jnp.where(tile_lane == p, tile, 0.0), axis=1, keepdims=True)
            f1 = jnp.sum(jnp.where(tile_lane == p + 1, tile, 0.0), axis=1, keepdims=True)
            tile = jnp.where((tile_lane == p) | (tile_lane == p + 1), 0.0, tile) - f0 * s_first - f1 * s_second
            tile = jnp.where(in_tile == 2 * u, s_first, jnp.where(in_tile == 2 * u + 1, s_second, tile))
        slab = [jnp.sum(jnp.where(in_tile == t, tile, 0.0), axis=0, keepdims=True) for t in range(8)]
        a = jnp.where((lane >= k) & (lane < k + 8), 0.0, a)
        for t in range(8):
            a = a - jnp.where(in_rows, 0.0, cols[t]) * slab[t]
        return jnp.where(in_rows, jnp.tile(tile, (size // 8, 1)), a)

    return lax.fori_loop(0, size // 8, step, block)


def _solve_kernel(m_ref, w_ref, y_ref, a_ref, *, block):
    n = m_ref.shape[0]
    a_ref[:, :n] = m_ref[...]
    a_ref[:, n:] = w_ref[...]
    blocks = n // block
    for j in range(blocks):
        lo = j * block
        hi = lo + block
        inverse = _invert_block(a_ref[lo:hi, lo:hi])
        pivot_rows = jnp.dot(inverse, a_ref[lo:hi, hi:], precision=HI,
                             preferred_element_type=jnp.float32)
        for i in range(blocks):
            if i == j:
                continue
            r = i * block
            a_ref[r:r + block, hi:] = a_ref[r:r + block, hi:] - jnp.dot(
                a_ref[r:r + block, lo:hi], pivot_rows, precision=HI,
                preferred_element_type=jnp.float32)
        a_ref[lo:hi, hi:] = pivot_rows
    y_ref[...] = a_ref[:, n:]


def spd_solve(system, rhs, block=128, interpret=False):
    n = system.shape[0]
    return pl.pallas_call(
        functools.partial(_solve_kernel, block=block),
        out_shape=jax.ShapeDtypeStruct(rhs.shape, jnp.float32),
        scratch_shapes=[pltpu.VMEM((n, n + rhs.shape[1]), jnp.float32)],
        interpret=interpret,
    )(system, rhs)


def partner(array, axis, bit):
    return lax.ppermute(array, axis, [(i, i ^ 1 << bit) for i in range(lax.axis_size(axis))])


def reduce_and_gather(value, order, position):
    bits = len(order)
    rows = value.shape[bits - 1:]
    remaining = [level for level in range(bits - 1, -1, -1) if level != order[0]]
    for level in order[1:-1]:
        axis = remaining.index(level)
        own_bit = position // 2**level % 2
        kept = lax.dynamic_index_in_dim(value, own_bit, axis=axis, keepdims=False)
        sent = lax.dynamic_index_in_dim(value, 1 - own_bit, axis=axis, keepdims=False)
        value = kept + partner(sent, "ex", level)
        remaining.remove(level)
    last = order[-1]
    value = value + partner(value, "ex", last)
    own = lax.dynamic_index_in_dim(value, position // 2**last % 2, axis=0, keepdims=False)
    present = [last]
    for level in reversed(order[:-1]):
        received = partner(value, "ex", level)
        high_side = position // 2**level % 2 == 1
        low = jnp.where(high_side, received, value)
        high = jnp.where(high_side, value, received)
        present.append(level)
        present.sort(reverse=True)
        value = jnp.stack([low, high], axis=present.index(level))
    return own, value.reshape((-1,) + rows[1:])


def bit_orders(bits):
    first = list(range(bits))
    if bits < 4:
        return [first]
    rest = list(range(4, bits))
    return [[0, 1, 2, 3] + rest, [0, 2, 1, 3] + rest, [0, 1, 3, 2] + rest, [0, 2, 3, 1] + rest]


def on_device(grads, proj, target_ids, target_counts):
    count_ex = lax.axis_size("ex")
    bits = count_ex.bit_length() - 1
    position = lax.axis_index("ex")
    ex_rows = grads.shape[0]
    examples = ex_rows * count_ex
    sketch_width = proj.shape[1]
    chips = count_ex // 2
    own_low = position % 2
    block_rows = proj.shape[0]
    with jax.named_scope("projection_pair"):
        sibling = partner(proj, "ex", 0)
        low_rows = jnp.where(own_low == 0, proj, sibling)
        high_rows = jnp.where(own_low == 0, sibling, proj)
    with jax.named_scope("gradient_exchange"):
        columns = lax.all_to_all(
            grads, "ex", split_axis=1, concat_axis=0, tiled=True,
            axis_index_groups=[[2 * chip + core for chip in range(chips)] for core in range(2)],
        )
    with jax.named_scope("partial_projection"):
        partial_value = jnp.dot(
            columns[:, :block_rows], low_rows, preferred_element_type=jnp.float32
        ) + jnp.dot(columns[:, block_rows:], high_rows, preferred_element_type=jnp.float32)
    orders = bit_orders(bits)
    width = sketch_width // len(orders)
    owned, gathered = [], []
    for half, order in enumerate(orders):
        with jax.named_scope("sketch_reduce_gather"):
            part, every = reduce_and_gather(
                partial_value[:, half * width:(half + 1) * width].reshape(
                    (2,) * (bits - 1) + (ex_rows, width)
                ),
                order,
                position,
            )
        gathered.append(every)
        owned.append(part)
    sketch = jnp.concatenate(owned, axis=1)
    sketch_all = jnp.concatenate(gathered, axis=1)
    slot_count = target_ids.shape[1]
    live_slot = jnp.arange(slot_count, dtype=jnp.int32)[None, :] < target_counts[:, None]
    example_index = jnp.arange(examples, dtype=jnp.int32)
    matches = (target_ids[:, :, None] == example_index[None, None, :]) & live_slot[:, :, None]
    weight = jnp.sum(matches.astype(jnp.float32), axis=1) / target_counts[:, None].astype(
        jnp.float32
    )
    if examples < sketch_width and examples % 128 == 0:
        with jax.named_scope("kernel_matrix"):
            kernel = jnp.dot(sketch_all, sketch_all.T, precision=lax.Precision.HIGHEST)
        with jax.named_scope("kernel_solve"):
            system = kernel / jnp.float32(examples) + 0.1 * jnp.eye(examples, dtype=jnp.float32)
            lanes = -(-weight.shape[0] // 128) * 128
            rhs = jnp.pad(weight.T, ((0, 0), (0, lanes - weight.shape[0])))
            coeffs = spd_solve(system, rhs, block=min(128, examples))[:, : weight.shape[0]]
        own_weight = lax.dynamic_slice_in_dim(weight.T, position * ex_rows, ex_rows, axis=0)
        own_coeffs = lax.dynamic_slice_in_dim(coeffs, position * ex_rows, ex_rows, axis=0)
        scores = jnp.float32(examples) * (own_weight - 0.1 * own_coeffs)
    else:
        with jax.named_scope("gram_solve"):
            gram_matrix = jnp.dot(sketch_all.T, sketch_all, precision=lax.Precision.HIGHEST)
            domain = jnp.dot(weight, sketch_all, precision=lax.Precision.HIGHEST)
            hessian = gram_matrix / jnp.float32(examples) + 0.1 * jnp.eye(
                sketch_width, dtype=jnp.float32
            )
            factor = jnp.linalg.cholesky(hessian)
            middle = lax.linalg.triangular_solve(factor, domain.T, left_side=True, lower=True)
            solved = lax.linalg.triangular_solve(
                factor, middle, left_side=True, lower=True, transpose_a=True
            )
        scores = jnp.dot(sketch, solved, precision=lax.Precision.HIGHEST)
    return (scores, sketch)


def solution(mesh):
    placed = (P(("groups", "ex"), None), P("ex", None), P(), P())
    return jax.shard_map(
        on_device,
        mesh=mesh,
        in_specs=placed,
        out_specs=(P(("groups", "ex"), None), P(("groups", "ex"), None)),
        check_vma=False,
    )
```

```python
import jax
import jax.numpy as jnp
from jax import lax
from jax.sharding import PartitionSpec as P
import functools
from jax.experimental import pallas as pl
from jax.experimental.pallas import tpu as pltpu

HI = lax.Precision.HIGHEST

def _invert_block(block):
    size = block.shape[0]
    lane = lax.broadcasted_iota(jnp.int32, block.shape, 1)
    sub = lax.broadcasted_iota(jnp.int32, block.shape, 0)
    lane_row = lax.broadcasted_iota(jnp.int32, (1, size), 1)
    sub_col = lax.broadcasted_iota(jnp.int32, (size, 1), 0)

    def pick(row, k):
        return jnp.sum(jnp.where(lane_row == k, row, 0.0), axis=1, keepdims=True)

    def pair_pivot(first, second, k):
        p00 = pick(first, k)
        p01 = pick(first, k + 1)
        p10 = pick(second, k)
        p11 = pick(second, k + 1)
        det = p00 * p11 - p01 * p10
        ident0 = jnp.where(lane_row == k, 1.0, jnp.where(lane_row == k + 1, 0.0, first))
        ident1 = jnp.where(lane_row == k, 0.0, jnp.where(lane_row == k + 1, 1.0, second))
        scaled0 = (p11 * ident0 - p01 * ident1) / det
        scaled1 = (p00 * ident1 - p10 * ident0) / det
        return scaled0, scaled1

    def eliminate(row, k, scaled0, scaled1):
        f0 = pick(row, k)
        f1 = pick(row, k + 1)
        kept = jnp.where((lane_row == k) | (lane_row == k + 1), 0.0, row)
        return kept - f0 * scaled0 - f1 * scaled1

    in_tile = lax.broadcasted_iota(jnp.int32, (8, size), 0)
    tile_lane = lax.broadcasted_iota(jnp.int32, (8, size), 1)

    def step(h, a):
        k = 8 * h
        in_rows = (sub >= k) & (sub < k + 8)
        tile = jnp.sum(jnp.where(in_rows, a, 0.0).reshape(size // 8, 8, size), axis=0)
        cols = [jnp.sum(jnp.where(lane == k + t, a, 0.0), axis=1, keepdims=True) for t in range(8)]
        for u in range(4):
            p = k + 2 * u
            first = jnp.sum(jnp.where(in_tile == 2 * u, tile, 0.0), axis=0, keepdims=True)
            second = jnp.sum(jnp.where(in_tile == 2 * u + 1, tile, 0.0), axis=0, keepdims=True)
            s_first, s_second = pair_pivot(first, second, p)
            f0 = jnp.sum(jnp.where(tile_lane == p, tile, 0.0), axis=1, keepdims=True)
            f1 = jnp.sum(jnp.where(tile_lane == p + 1, tile, 0.0), axis=1, keepdims=True)
            tile = jnp.where((tile_lane == p) | (tile_lane == p + 1), 0.0, tile) - f0 * s_first - f1 * s_second
            tile = jnp.where(in_tile == 2 * u, s_first, jnp.where(in_tile == 2 * u + 1, s_second, tile))
        slab = [jnp.sum(jnp.where(in_tile == t, tile, 0.0), axis=0, keepdims=True) for t in range(8)]
        a = jnp.where((lane >= k) & (lane < k + 8), 0.0, a)
        for t in range(8):
            a = a - jnp.where(in_rows, 0.0, cols[t]) * slab[t]
        return jnp.where(in_rows, jnp.tile(tile, (size // 8, 1)), a)

    return lax.fori_loop(0, size // 8, step, block)


def _solve_kernel(m_ref, w_ref, y_ref, a_ref, *, block):
    n = m_ref.shape[0]
    a_ref[:, :n] = m_ref[...]
    a_ref[:, n:] = w_ref[...]
    blocks = n // block
    for j in range(blocks):
        lo = j * block
        hi = lo + block
        inverse = _invert_block(a_ref[lo:hi, lo:hi])
        pivot_rows = jnp.dot(inverse, a_ref[lo:hi, hi:], precision=HI,
                             preferred_element_type=jnp.float32)
        for i in range(blocks):
            if i == j:
                continue
            r = i * block
            a_ref[r:r + block, hi:] = a_ref[r:r + block, hi:] - jnp.dot(
                a_ref[r:r + block, lo:hi], pivot_rows, precision=HI,
                preferred_element_type=jnp.float32)
        a_ref[lo:hi, hi:] = pivot_rows
    y_ref[...] = a_ref[:, n:]


def spd_solve(system, rhs, block=128, interpret=False):
    n = system.shape[0]
    return pl.pallas_call(
        functools.partial(_solve_kernel, block=block),
        out_shape=jax.ShapeDtypeStruct(rhs.shape, jnp.float32),
        scratch_shapes=[pltpu.VMEM((n, n + rhs.shape[1]), jnp.float32)],
        interpret=interpret,
    )(system, rhs)


def partner(array, axis, bit):
    return lax.ppermute(array, axis, [(i, i ^ 1 << bit) for i in range(lax.axis_size(axis))])


def reduce_and_gather(value, order, position):
    bits = len(order)
    rows = value.shape[bits - 1:]
    remaining = [level for level in range(bits - 1, -1, -1) if level != order[0]]
    for level in order[1:-1]:
        axis = remaining.index(level)
        own_bit = position // 2**level % 2
        kept = lax.dynamic_index_in_dim(value, own_bit, axis=axis, keepdims=False)
        sent = lax.dynamic_index_in_dim(value, 1 - own_bit, axis=axis, keepdims=False)
        value = kept + partner(sent, "ex", level)
        remaining.remove(level)
    last = order[-1]
    value = value + partner(value, "ex", last)
    own = lax.dynamic_index_in_dim(value, position // 2**last % 2, axis=0, keepdims=False)
    present = [last]
    for level in reversed(order[:-1]):
        received = partner(value, "ex", level)
        high_side = position // 2**level % 2 == 1
        low = jnp.where(high_side, received, value)
        high = jnp.where(high_side, value, received)
        present.append(level)
        present.sort(reverse=True)
        value = jnp.stack([low, high], axis=present.index(level))
    return own, value.reshape((-1,) + rows[1:])


def bit_orders(bits):
    first = list(range(bits))
    if bits < 4:
        return [first]
    rest = list(range(4, bits))
    return [[0, 1, 2, 3] + rest, [0, 2, 1, 3] + rest, [0, 1, 3, 2] + rest, [0, 2, 3, 1] + rest]


def on_device(grads, proj, target_ids, target_counts):
    count_ex = lax.axis_size("ex")
    bits = count_ex.bit_length() - 1
    position = lax.axis_index("ex")
    ex_rows = grads.shape[0]
    examples = ex_rows * count_ex
    sketch_width = proj.shape[1]
    chips = count_ex // 2
    own_low = position % 2
    block_rows = proj.shape[0]
    with jax.named_scope("projection_pair"):
        sibling = partner(proj, "ex", 0)
        low_rows = jnp.where(own_low == 0, proj, sibling)
        high_rows = jnp.where(own_low == 0, sibling, proj)
    with jax.named_scope("gradient_exchange"):
        columns = lax.all_to_all(
            grads, "ex", split_axis=1, concat_axis=0, tiled=True,
            axis_index_groups=[[2 * chip + core for chip in range(chips)] for core in range(2)],
        )
    columns, low_rows, high_rows = lax.optimization_barrier((columns, low_rows, high_rows))
    with jax.named_scope("partial_projection"):
        partial_value = jnp.dot(
            columns[:, :block_rows], low_rows, preferred_element_type=jnp.float32
        ) + jnp.dot(columns[:, block_rows:], high_rows, preferred_element_type=jnp.float32)
    orders = bit_orders(bits)
    width = sketch_width // len(orders)
    owned, gathered = [], []
    for half, order in enumerate(orders):
        with jax.named_scope("sketch_reduce_gather"):
            part, every = reduce_and_gather(
                partial_value[:, half * width:(half + 1) * width].reshape(
                    (2,) * (bits - 1) + (ex_rows, width)
                ),
                order,
                position,
            )
        gathered.append(every)
        owned.append(part)
    sketch = jnp.concatenate(owned, axis=1)
    sketch_all = jnp.concatenate(gathered, axis=1)
    slot_count = target_ids.shape[1]
    live_slot = jnp.arange(slot_count, dtype=jnp.int32)[None, :] < target_counts[:, None]
    example_index = jnp.arange(examples, dtype=jnp.int32)
    matches = (target_ids[:, :, None] == example_index[None, None, :]) & live_slot[:, :, None]
    weight = jnp.sum(matches.astype(jnp.float32), axis=1) / target_counts[:, None].astype(
        jnp.float32
    )
    if examples < sketch_width and examples % 128 == 0:
        with jax.named_scope("kernel_matrix"):
            kernel = jnp.dot(sketch_all, sketch_all.T, precision=lax.Precision.HIGHEST)
        with jax.named_scope("kernel_solve"):
            system = kernel / jnp.float32(examples) + 0.1 * jnp.eye(examples, dtype=jnp.float32)
            lanes = -(-weight.shape[0] // 128) * 128
            rhs = jnp.pad(weight.T, ((0, 0), (0, lanes - weight.shape[0])))
            coeffs = spd_solve(system, rhs, block=min(128, examples))[:, : weight.shape[0]]
        own_weight = lax.dynamic_slice_in_dim(weight.T, position * ex_rows, ex_rows, axis=0)
        own_coeffs = lax.dynamic_slice_in_dim(coeffs, position * ex_rows, ex_rows, axis=0)
        scores = jnp.float32(examples) * (own_weight - 0.1 * own_coeffs)
    else:
        with jax.named_scope("gram_solve"):
            gram_matrix = jnp.dot(sketch_all.T, sketch_all, precision=lax.Precision.HIGHEST)
            domain = jnp.dot(weight, sketch_all, precision=lax.Precision.HIGHEST)
            hessian = gram_matrix / jnp.float32(examples) + 0.1 * jnp.eye(
                sketch_width, dtype=jnp.float32
            )
            factor = jnp.linalg.cholesky(hessian)
            middle = lax.linalg.triangular_solve(factor, domain.T, left_side=True, lower=True)
            solved = lax.linalg.triangular_solve(
                factor, middle, left_side=True, lower=True, transpose_a=True
            )
        scores = jnp.dot(sketch, solved, precision=lax.Precision.HIGHEST)
    return (scores, sketch)


def solution(mesh):
    placed = (P(("groups", "ex"), None), P("ex", None), P(), P())
    return jax.shard_map(
        on_device,
        mesh=mesh,
        in_specs=placed,
        out_specs=(P(("groups", "ex"), None), P(("groups", "ex"), None)),
        check_vma=False,
    )
```

```python
import jax
import jax.numpy as jnp
from jax import lax
from jax.sharding import PartitionSpec as P
import functools
from jax.experimental import pallas as pl
from jax.experimental.pallas import tpu as pltpu

HI = lax.Precision.HIGHEST

def _invert_block(block):
    size = block.shape[0]
    lane = lax.broadcasted_iota(jnp.int32, block.shape, 1)
    sub = lax.broadcasted_iota(jnp.int32, block.shape, 0)
    lane_row = lax.broadcasted_iota(jnp.int32, (1, size), 1)
    sub_col = lax.broadcasted_iota(jnp.int32, (size, 1), 0)

    def pick(row, k):
        return jnp.sum(jnp.where(lane_row == k, row, 0.0), axis=1, keepdims=True)

    def pair_pivot(first, second, k):
        p00 = pick(first, k)
        p01 = pick(first, k + 1)
        p10 = pick(second, k)
        p11 = pick(second, k + 1)
        det = p00 * p11 - p01 * p10
        ident0 = jnp.where(lane_row == k, 1.0, jnp.where(lane_row == k + 1, 0.0, first))
        ident1 = jnp.where(lane_row == k, 0.0, jnp.where(lane_row == k + 1, 1.0, second))
        scaled0 = (p11 * ident0 - p01 * ident1) / det
        scaled1 = (p00 * ident1 - p10 * ident0) / det
        return scaled0, scaled1

    def eliminate(row, k, scaled0, scaled1):
        f0 = pick(row, k)
        f1 = pick(row, k + 1)
        kept = jnp.where((lane_row == k) | (lane_row == k + 1), 0.0, row)
        return kept - f0 * scaled0 - f1 * scaled1

    in_tile = lax.broadcasted_iota(jnp.int32, (8, size), 0)
    tile_lane = lax.broadcasted_iota(jnp.int32, (8, size), 1)

    def step(h, a):
        k = 8 * h
        in_rows = (sub >= k) & (sub < k + 8)
        tile = jnp.sum(jnp.where(in_rows, a, 0.0).reshape(size // 8, 8, size), axis=0)
        cols = [jnp.sum(jnp.where(lane == k + t, a, 0.0), axis=1, keepdims=True) for t in range(8)]
        for u in range(4):
            p = k + 2 * u
            first = jnp.sum(jnp.where(in_tile == 2 * u, tile, 0.0), axis=0, keepdims=True)
            second = jnp.sum(jnp.where(in_tile == 2 * u + 1, tile, 0.0), axis=0, keepdims=True)
            s_first, s_second = pair_pivot(first, second, p)
            f0 = jnp.sum(jnp.where(tile_lane == p, tile, 0.0), axis=1, keepdims=True)
            f1 = jnp.sum(jnp.where(tile_lane == p + 1, tile, 0.0), axis=1, keepdims=True)
            tile = jnp.where((tile_lane == p) | (tile_lane == p + 1), 0.0, tile) - f0 * s_first - f1 * s_second
            tile = jnp.where(in_tile == 2 * u, s_first, jnp.where(in_tile == 2 * u + 1, s_second, tile))
        slab = [jnp.sum(jnp.where(in_tile == t, tile, 0.0), axis=0, keepdims=True) for t in range(8)]
        a = jnp.where((lane >= k) & (lane < k + 8), 0.0, a)
        for t in range(8):
            a = a - jnp.where(in_rows, 0.0, cols[t]) * slab[t]
        return jnp.where(in_rows, jnp.tile(tile, (size // 8, 1)), a)

    return lax.fori_loop(0, size // 8, step, block)


def _solve_kernel(m_ref, w_ref, y_ref, a_ref, *, block):
    n = m_ref.shape[0]
    a_ref[:, :n] = m_ref[...]
    a_ref[:, n:] = w_ref[...]
    blocks = n // block
    for j in range(blocks):
        lo = j * block
        hi = lo + block
        inverse = _invert_block(a_ref[lo:hi, lo:hi])
        pivot_rows = jnp.dot(inverse, a_ref[lo:hi, hi:], precision=HI,
                             preferred_element_type=jnp.float32)
        for i in range(blocks):
            if i == j:
                continue
            r = i * block
            a_ref[r:r + block, hi:] = a_ref[r:r + block, hi:] - jnp.dot(
                a_ref[r:r + block, lo:hi], pivot_rows, precision=HI,
                preferred_element_type=jnp.float32)
        a_ref[lo:hi, hi:] = pivot_rows
    y_ref[...] = a_ref[:, n:]


def spd_solve(system, rhs, block=128, interpret=False):
    n = system.shape[0]
    return pl.pallas_call(
        functools.partial(_solve_kernel, block=block),
        out_shape=jax.ShapeDtypeStruct(rhs.shape, jnp.float32),
        scratch_shapes=[pltpu.VMEM((n, n + rhs.shape[1]), jnp.float32)],
        interpret=interpret,
    )(system, rhs)


def partner(array, axis, bit):
    return lax.ppermute(array, axis, [(i, i ^ 1 << bit) for i in range(lax.axis_size(axis))])


def reduce_and_gather(partial_value, order, position):
    bits = len(order)
    rows = partial_value.shape[1:]
    value = partial_value.reshape((2,) * bits + rows)
    remaining = list(range(bits - 1, -1, -1))
    for level in order[:-1]:
        axis = remaining.index(level)
        own_bit = position // 2**level % 2
        kept = lax.dynamic_index_in_dim(value, own_bit, axis=axis, keepdims=False)
        sent = lax.dynamic_index_in_dim(value, 1 - own_bit, axis=axis, keepdims=False)
        value = kept + partner(sent, "ex", level)
        remaining.remove(level)
    last = order[-1]
    value = value + partner(value, "ex", last)
    own = lax.dynamic_index_in_dim(value, position // 2**last % 2, axis=0, keepdims=False)
    present = [last]
    for level in reversed(order[:-1]):
        received = partner(value, "ex", level)
        high_side = position // 2**level % 2 == 1
        low = jnp.where(high_side, received, value)
        high = jnp.where(high_side, value, received)
        present.append(level)
        present.sort(reverse=True)
        value = jnp.stack([low, high], axis=present.index(level))
    return own, value.reshape((-1,) + rows[1:])


def bit_orders(bits):
    first = list(range(bits))
    if bits < 4:
        return [first]
    rest = list(range(4, bits))
    return [order + rest for order in (
        [0, 1, 2, 3], [0, 2, 1, 3], [0, 1, 3, 2], [0, 2, 3, 1],
        [0, 3, 1, 2], [0, 3, 2, 1], [0, 1, 2, 3], [0, 2, 1, 3])]


def on_device(grads, proj, target_ids, target_counts):
    count_ex = lax.axis_size("ex")
    bits = count_ex.bit_length() - 1
    position = lax.axis_index("ex")
    ex_rows = grads.shape[0]
    examples = ex_rows * count_ex
    sketch_width = proj.shape[1]
    with jax.named_scope("gradient_exchange"):
        columns = lax.all_to_all(grads, "ex", split_axis=1, concat_axis=0, tiled=True)
    with jax.named_scope("partial_projection"):
        partial_value = jnp.dot(columns, proj, preferred_element_type=jnp.float32)
    orders = bit_orders(bits)
    width = sketch_width // len(orders)
    owned, gathered = [], []
    for half, order in enumerate(orders):
        with jax.named_scope("sketch_reduce_gather"):
            part, every = reduce_and_gather(
                partial_value[:, half * width:(half + 1) * width].reshape(
                    count_ex, ex_rows, width
                ),
                order,
                position,
            )
        gathered.append(every)
        owned.append(part)
    sketch = jnp.concatenate(owned, axis=1)
    sketch_all = jnp.concatenate(gathered, axis=1)
    slot_count = target_ids.shape[1]
    live_slot = jnp.arange(slot_count, dtype=jnp.int32)[None, :] < target_counts[:, None]
    example_index = jnp.arange(examples, dtype=jnp.int32)
    matches = (target_ids[:, :, None] == example_index[None, None, :]) & live_slot[:, :, None]
    weight = jnp.sum(matches.astype(jnp.float32), axis=1) / target_counts[:, None].astype(
        jnp.float32
    )
    if examples < sketch_width and examples % 128 == 0:
        with jax.named_scope("kernel_matrix"):
            kernel = jnp.dot(sketch_all, sketch_all.T, precision=lax.Precision.HIGHEST)
        with jax.named_scope("kernel_solve"):
            system = kernel / jnp.float32(examples) + 0.1 * jnp.eye(examples, dtype=jnp.float32)
            lanes = -(-weight.shape[0] // 128) * 128
            rhs = jnp.pad(weight.T, ((0, 0), (0, lanes - weight.shape[0])))
            coeffs = spd_solve(system, rhs, block=min(128, examples))[:, : weight.shape[0]]
        own_weight = lax.dynamic_slice_in_dim(weight.T, position * ex_rows, ex_rows, axis=0)
        own_coeffs = lax.dynamic_slice_in_dim(coeffs, position * ex_rows, ex_rows, axis=0)
        scores = jnp.float32(examples) * (own_weight - 0.1 * own_coeffs)
    else:
        with jax.named_scope("gram_solve"):
            gram_matrix = jnp.dot(sketch_all.T, sketch_all, precision=lax.Precision.HIGHEST)
            domain = jnp.dot(weight, sketch_all, precision=lax.Precision.HIGHEST)
            hessian = gram_matrix / jnp.float32(examples) + 0.1 * jnp.eye(
                sketch_width, dtype=jnp.float32
            )
            factor = jnp.linalg.cholesky(hessian)
            middle = lax.linalg.triangular_solve(factor, domain.T, left_side=True, lower=True)
            solved = lax.linalg.triangular_solve(
                factor, middle, left_side=True, lower=True, transpose_a=True
            )
        scores = jnp.dot(sketch, solved, precision=lax.Precision.HIGHEST)
    return (scores, sketch)


def solution(mesh):
    placed = (P(("groups", "ex"), None), P("ex", None), P(), P())
    return jax.shard_map(
        on_device,
        mesh=mesh,
        in_specs=placed,
        out_specs=(P(("groups", "ex"), None), P(("groups", "ex"), None)),
        check_vma=False,
    )
```

```python
import jax
import jax.numpy as jnp
from jax import lax
from jax.sharding import PartitionSpec as P
import functools
from jax.experimental import pallas as pl
from jax.experimental.pallas import tpu as pltpu

HI = lax.Precision.HIGHEST

def _invert_block(block):
    size = block.shape[0]
    lane = lax.broadcasted_iota(jnp.int32, block.shape, 1)
    sub = lax.broadcasted_iota(jnp.int32, block.shape, 0)
    lane_row = lax.broadcasted_iota(jnp.int32, (1, size), 1)
    sub_col = lax.broadcasted_iota(jnp.int32, (size, 1), 0)

    def pick(row, k):
        return jnp.sum(jnp.where(lane_row == k, row, 0.0), axis=1, keepdims=True)

    def pair_pivot(first, second, k):
        p00 = pick(first, k)
        p01 = pick(first, k + 1)
        p10 = pick(second, k)
        p11 = pick(second, k + 1)
        det = p00 * p11 - p01 * p10
        ident0 = jnp.where(lane_row == k, 1.0, jnp.where(lane_row == k + 1, 0.0, first))
        ident1 = jnp.where(lane_row == k, 0.0, jnp.where(lane_row == k + 1, 1.0, second))
        scaled0 = (p11 * ident0 - p01 * ident1) / det
        scaled1 = (p00 * ident1 - p10 * ident0) / det
        return scaled0, scaled1

    def eliminate(row, k, scaled0, scaled1):
        f0 = pick(row, k)
        f1 = pick(row, k + 1)
        kept = jnp.where((lane_row == k) | (lane_row == k + 1), 0.0, row)
        return kept - f0 * scaled0 - f1 * scaled1

    in_tile = lax.broadcasted_iota(jnp.int32, (8, size), 0)
    tile_lane = lax.broadcasted_iota(jnp.int32, (8, size), 1)

    def step(h, a):
        k = 8 * h
        in_rows = (sub >= k) & (sub < k + 8)
        tile = jnp.sum(jnp.where(in_rows, a, 0.0).reshape(size // 8, 8, size), axis=0)
        cols = [jnp.sum(jnp.where(lane == k + t, a, 0.0), axis=1, keepdims=True) for t in range(8)]
        for u in range(4):
            p = k + 2 * u
            first = jnp.sum(jnp.where(in_tile == 2 * u, tile, 0.0), axis=0, keepdims=True)
            second = jnp.sum(jnp.where(in_tile == 2 * u + 1, tile, 0.0), axis=0, keepdims=True)
            s_first, s_second = pair_pivot(first, second, p)
            f0 = jnp.sum(jnp.where(tile_lane == p, tile, 0.0), axis=1, keepdims=True)
            f1 = jnp.sum(jnp.where(tile_lane == p + 1, tile, 0.0), axis=1, keepdims=True)
            tile = jnp.where((tile_lane == p) | (tile_lane == p + 1), 0.0, tile) - f0 * s_first - f1 * s_second
            tile = jnp.where(in_tile == 2 * u, s_first, jnp.where(in_tile == 2 * u + 1, s_second, tile))
        slab = [jnp.sum(jnp.where(in_tile == t, tile, 0.0), axis=0, keepdims=True) for t in range(8)]
        a = jnp.where((lane >= k) & (lane < k + 8), 0.0, a)
        for t in range(8):
            a = a - jnp.where(in_rows, 0.0, cols[t]) * slab[t]
        return jnp.where(in_rows, jnp.tile(tile, (size // 8, 1)), a)

    return lax.fori_loop(0, size // 8, step, block)


def _solve_kernel(m_ref, w_ref, y_ref, a_ref, *, block):
    n = m_ref.shape[0]
    a_ref[:, :n] = m_ref[...]
    a_ref[:, n:] = w_ref[...]
    blocks = n // block
    for j in range(blocks):
        lo = j * block
        hi = lo + block
        inverse = _invert_block(a_ref[lo:hi, lo:hi])
        pivot_rows = jnp.dot(inverse, a_ref[lo:hi, hi:], precision=HI,
                             preferred_element_type=jnp.float32)
        for i in range(blocks):
            if i == j:
                continue
            r = i * block
            a_ref[r:r + block, hi:] = a_ref[r:r + block, hi:] - jnp.dot(
                a_ref[r:r + block, lo:hi], pivot_rows, precision=HI,
                preferred_element_type=jnp.float32)
        a_ref[lo:hi, hi:] = pivot_rows
    y_ref[...] = a_ref[:, n:]


def spd_solve(system, rhs, block=128, interpret=False):
    n = system.shape[0]
    return pl.pallas_call(
        functools.partial(_solve_kernel, block=block),
        out_shape=jax.ShapeDtypeStruct(rhs.shape, jnp.float32),
        scratch_shapes=[pltpu.VMEM((n, n + rhs.shape[1]), jnp.float32)],
        interpret=interpret,
    )(system, rhs)


def partner(array, axis, bit):
    return lax.ppermute(array, axis, [(i, i ^ 1 << bit) for i in range(lax.axis_size(axis))])


def reduce_and_gather(partial_value, order, position):
    bits = len(order)
    rows = partial_value.shape[1:]
    value = partial_value.reshape((2,) * bits + rows)
    remaining = list(range(bits - 1, -1, -1))
    for level in order[:-1]:
        axis = remaining.index(level)
        own_bit = position // 2**level % 2
        kept = lax.dynamic_index_in_dim(value, own_bit, axis=axis, keepdims=False)
        sent = lax.dynamic_index_in_dim(value, 1 - own_bit, axis=axis, keepdims=False)
        value = kept + partner(sent, "ex", level)
        remaining.remove(level)
    last = order[-1]
    value = value + partner(value, "ex", last)
    own = lax.dynamic_index_in_dim(value, position // 2**last % 2, axis=0, keepdims=False)
    present = [last]
    for level in reversed(order[:-1]):
        received = partner(value, "ex", level)
        high_side = position // 2**level % 2 == 1
        low = jnp.where(high_side, received, value)
        high = jnp.where(high_side, value, received)
        present.append(level)
        present.sort(reverse=True)
        value = jnp.stack([low, high], axis=present.index(level))
    return own, value.reshape((-1,) + rows[1:])


def bit_orders(bits):
    first = list(range(bits))
    if bits < 4:
        return [first]
    rest = list(range(4, bits))
    return [[0, 1, 2, 3] + rest, [0, 2, 1, 3] + rest, [0, 1, 2, 3] + rest, [0, 2, 1, 3] + rest]


def on_device(grads, proj, target_ids, target_counts):
    count_ex = lax.axis_size("ex")
    bits = count_ex.bit_length() - 1
    position = lax.axis_index("ex")
    ex_rows = grads.shape[0]
    examples = ex_rows * count_ex
    sketch_width = proj.shape[1]
    with jax.named_scope("gradient_exchange"):
        columns = lax.all_to_all(grads, "ex", split_axis=1, concat_axis=0, tiled=True)
    with jax.named_scope("partial_projection"):
        partial_value = jnp.dot(columns, proj, preferred_element_type=jnp.float32)
    orders = bit_orders(bits)
    width = sketch_width // len(orders)
    owned, gathered = [], []
    for half, order in enumerate(orders):
        with jax.named_scope("sketch_reduce_gather"):
            part, every = reduce_and_gather(
                partial_value[:, half * width:(half + 1) * width].reshape(
                    count_ex, ex_rows, width
                ),
                order,
                position,
            )
        gathered.append(every)
        owned.append(part)
    sketch = jnp.concatenate(owned, axis=1)
    sketch_all = jnp.concatenate(gathered, axis=1)
    slot_count = target_ids.shape[1]
    live_slot = jnp.arange(slot_count, dtype=jnp.int32)[None, :] < target_counts[:, None]
    example_index = jnp.arange(examples, dtype=jnp.int32)
    matches = (target_ids[:, :, None] == example_index[None, None, :]) & live_slot[:, :, None]
    weight = jnp.sum(matches.astype(jnp.float32), axis=1) / target_counts[:, None].astype(
        jnp.float32
    )
    if examples < sketch_width and examples % 128 == 0:
        with jax.named_scope("kernel_matrix"):
            kernel = jnp.dot(sketch_all, sketch_all.T, precision=lax.Precision.HIGHEST)
        with jax.named_scope("kernel_solve"):
            system = kernel / jnp.float32(examples) + 0.1 * jnp.eye(examples, dtype=jnp.float32)
            lanes = -(-weight.shape[0] // 128) * 128
            rhs = jnp.pad(weight.T, ((0, 0), (0, lanes - weight.shape[0])))
            coeffs = spd_solve(system, rhs, block=min(128, examples))[:, : weight.shape[0]]
        own_weight = lax.dynamic_slice_in_dim(weight.T, position * ex_rows, ex_rows, axis=0)
        own_coeffs = lax.dynamic_slice_in_dim(coeffs, position * ex_rows, ex_rows, axis=0)
        scores = jnp.float32(examples) * (own_weight - 0.1 * own_coeffs)
    else:
        with jax.named_scope("gram_solve"):
            gram_matrix = jnp.dot(sketch_all.T, sketch_all, precision=lax.Precision.HIGHEST)
            domain = jnp.dot(weight, sketch_all, precision=lax.Precision.HIGHEST)
            hessian = gram_matrix / jnp.float32(examples) + 0.1 * jnp.eye(
                sketch_width, dtype=jnp.float32
            )
            factor = jnp.linalg.cholesky(hessian)
            middle = lax.linalg.triangular_solve(factor, domain.T, left_side=True, lower=True)
            solved = lax.linalg.triangular_solve(
                factor, middle, left_side=True, lower=True, transpose_a=True
            )
        scores = jnp.dot(sketch, solved, precision=lax.Precision.HIGHEST)
    return (scores, sketch)


def solution(mesh):
    placed = (P(("groups", "ex"), None), P("ex", None), P(), P())
    return jax.shard_map(
        on_device,
        mesh=mesh,
        in_specs=placed,
        out_specs=(P(("groups", "ex"), None), P(("groups", "ex"), None)),
        check_vma=False,
    )
```

```python
import jax
import jax.numpy as jnp
from jax import lax
from jax.sharding import PartitionSpec as P
import functools
from jax.experimental import pallas as pl
from jax.experimental.pallas import tpu as pltpu

HI = lax.Precision.HIGHEST

def _invert_block(block):
    size = block.shape[0]
    lane = lax.broadcasted_iota(jnp.int32, block.shape, 1)
    sub = lax.broadcasted_iota(jnp.int32, block.shape, 0)
    lane_row = lax.broadcasted_iota(jnp.int32, (1, size), 1)
    sub_col = lax.broadcasted_iota(jnp.int32, (size, 1), 0)

    def pick(row, k):
        return jnp.sum(jnp.where(lane_row == k, row, 0.0), axis=1, keepdims=True)

    def pair_pivot(first, second, k):
        p00 = pick(first, k)
        p01 = pick(first, k + 1)
        p10 = pick(second, k)
        p11 = pick(second, k + 1)
        det = p00 * p11 - p01 * p10
        ident0 = jnp.where(lane_row == k, 1.0, jnp.where(lane_row == k + 1, 0.0, first))
        ident1 = jnp.where(lane_row == k, 0.0, jnp.where(lane_row == k + 1, 1.0, second))
        scaled0 = (p11 * ident0 - p01 * ident1) / det
        scaled1 = (p00 * ident1 - p10 * ident0) / det
        return scaled0, scaled1

    def eliminate(row, k, scaled0, scaled1):
        f0 = pick(row, k)
        f1 = pick(row, k + 1)
        kept = jnp.where((lane_row == k) | (lane_row == k + 1), 0.0, row)
        return kept - f0 * scaled0 - f1 * scaled1

    in_tile = lax.broadcasted_iota(jnp.int32, (8, size), 0)
    tile_lane = lax.broadcasted_iota(jnp.int32, (8, size), 1)

    def step(h, a):
        k = 8 * h
        in_rows = (sub >= k) & (sub < k + 8)
        tile = jnp.sum(jnp.where(in_rows, a, 0.0).reshape(size // 8, 8, size), axis=0)
        cols = [jnp.sum(jnp.where(lane == k + t, a, 0.0), axis=1, keepdims=True) for t in range(8)]
        for u in range(4):
            p = k + 2 * u
            first = jnp.sum(jnp.where(in_tile == 2 * u, tile, 0.0), axis=0, keepdims=True)
            second = jnp.sum(jnp.where(in_tile == 2 * u + 1, tile, 0.0), axis=0, keepdims=True)
            s_first, s_second = pair_pivot(first, second, p)
            f0 = jnp.sum(jnp.where(tile_lane == p, tile, 0.0), axis=1, keepdims=True)
            f1 = jnp.sum(jnp.where(tile_lane == p + 1, tile, 0.0), axis=1, keepdims=True)
            tile = jnp.where((tile_lane == p) | (tile_lane == p + 1), 0.0, tile) - f0 * s_first - f1 * s_second
            tile = jnp.where(in_tile == 2 * u, s_first, jnp.where(in_tile == 2 * u + 1, s_second, tile))
        slab = [jnp.sum(jnp.where(in_tile == t, tile, 0.0), axis=0, keepdims=True) for t in range(8)]
        a = jnp.where((lane >= k) & (lane < k + 8), 0.0, a)
        for t in range(8):
            a = a - jnp.where(in_rows, 0.0, cols[t]) * slab[t]
        return jnp.where(in_rows, jnp.tile(tile, (size // 8, 1)), a)

    return lax.fori_loop(0, size // 8, step, block)


def _solve_kernel(m_ref, w_ref, y_ref, a_ref, *, block):
    n = m_ref.shape[0]
    a_ref[:, :n] = m_ref[...]
    a_ref[:, n:] = w_ref[...]
    blocks = n // block
    for j in range(blocks):
        lo = j * block
        hi = lo + block
        inverse = _invert_block(a_ref[lo:hi, lo:hi])
        pivot_rows = jnp.dot(inverse, a_ref[lo:hi, hi:], precision=HI,
                             preferred_element_type=jnp.float32)
        for i in range(blocks):
            if i == j:
                continue
            r = i * block
            a_ref[r:r + block, hi:] = a_ref[r:r + block, hi:] - jnp.dot(
                a_ref[r:r + block, lo:hi], pivot_rows, precision=HI,
                preferred_element_type=jnp.float32)
        a_ref[lo:hi, hi:] = pivot_rows
    y_ref[...] = a_ref[:, n:]


def spd_solve(system, rhs, block=128, interpret=False):
    n = system.shape[0]
    return pl.pallas_call(
        functools.partial(_solve_kernel, block=block),
        out_shape=jax.ShapeDtypeStruct(rhs.shape, jnp.float32),
        scratch_shapes=[pltpu.VMEM((n, n + rhs.shape[1]), jnp.float32)],
        interpret=interpret,
    )(system, rhs)


def partner(array, axis, bit):
    return lax.ppermute(array, axis, [(i, i ^ 1 << bit) for i in range(lax.axis_size(axis))])


def reduce_and_gather(partial_value, order, position):
    bits = len(order)
    rows = partial_value.shape[1:]
    value = partial_value.reshape((2,) * bits + rows)
    remaining = list(range(bits - 1, -1, -1))
    for level in order[:-1]:
        axis = remaining.index(level)
        own_bit = position // 2**level % 2
        kept = lax.dynamic_index_in_dim(value, own_bit, axis=axis, keepdims=False)
        sent = lax.dynamic_index_in_dim(value, 1 - own_bit, axis=axis, keepdims=False)
        value = kept + partner(sent, "ex", level)
        remaining.remove(level)
    last = order[-1]
    value = value + partner(value, "ex", last)
    own = lax.dynamic_index_in_dim(value, position // 2**last % 2, axis=0, keepdims=False)
    present = [last]
    for level in reversed(order[:-1]):
        received = partner(value, "ex", level)
        high_side = position // 2**level % 2 == 1
        low = jnp.where(high_side, received, value)
        high = jnp.where(high_side, value, received)
        present.append(level)
        present.sort(reverse=True)
        value = jnp.stack([low, high], axis=present.index(level))
    return own, value.reshape((-1,) + rows[1:])


def bit_orders(bits):
    first = list(range(bits))
    if bits < 4:
        return [first]
    rest = list(range(4, bits))
    return [[0, 1, 2, 3] + rest, [0, 2, 1, 3] + rest]


def on_device(grads, proj, target_ids, target_counts):
    count_ex = lax.axis_size("ex")
    bits = count_ex.bit_length() - 1
    position = lax.axis_index("ex")
    ex_rows = grads.shape[0]
    examples = ex_rows * count_ex
    sketch_width = proj.shape[1]
    with jax.named_scope("gradient_exchange"):
        columns = lax.all_to_all(grads, "ex", split_axis=1, concat_axis=0, tiled=True)
    with jax.named_scope("partial_projection"):
        partial_value = jnp.dot(columns, proj, preferred_element_type=jnp.float32)
    orders = bit_orders(bits)
    width = sketch_width // len(orders)
    owned, gathered = [], []
    for half, order in enumerate(orders):
        with jax.named_scope("sketch_reduce_gather"):
            part, every = reduce_and_gather(
                partial_value[:, half * width:(half + 1) * width].reshape(
                    count_ex, ex_rows, width
                ),
                order,
                position,
            )
        gathered.append(every)
        owned.append(part)
    sketch = jnp.concatenate(owned, axis=1)
    sketch_all = jnp.concatenate(gathered, axis=1)
    slot_count = target_ids.shape[1]
    live_slot = jnp.arange(slot_count, dtype=jnp.int32)[None, :] < target_counts[:, None]
    example_index = jnp.arange(examples, dtype=jnp.int32)
    matches = (target_ids[:, :, None] == example_index[None, None, :]) & live_slot[:, :, None]
    weight = jnp.sum(matches.astype(jnp.float32), axis=1) / target_counts[:, None].astype(
        jnp.float32
    )
    if examples < sketch_width and examples % 128 == 0:
        with jax.named_scope("kernel_matrix"):
            kernel = jnp.dot(sketch_all, sketch_all.T, precision=lax.Precision.HIGHEST)
        with jax.named_scope("kernel_solve"):
            system = kernel / jnp.float32(examples) + 0.1 * jnp.eye(examples, dtype=jnp.float32)
            lanes = -(-weight.shape[0] // 128) * 128
            rhs = jnp.pad(weight.T, ((0, 0), (0, lanes - weight.shape[0])))
            coeffs = spd_solve(system, rhs, block=min(128, examples))[:, : weight.shape[0]]
        own_weight = lax.dynamic_slice_in_dim(weight.T, position * ex_rows, ex_rows, axis=0)
        own_coeffs = lax.dynamic_slice_in_dim(coeffs, position * ex_rows, ex_rows, axis=0)
        scores = jnp.float32(examples) * (own_weight - 0.1 * own_coeffs)
    else:
        with jax.named_scope("gram_solve"):
            gram_matrix = jnp.dot(sketch_all.T, sketch_all, precision=lax.Precision.HIGHEST)
            domain = jnp.dot(weight, sketch_all, precision=lax.Precision.HIGHEST)
            hessian = gram_matrix / jnp.float32(examples) + 0.1 * jnp.eye(
                sketch_width, dtype=jnp.float32
            )
            factor = jnp.linalg.cholesky(hessian)
            middle = lax.linalg.triangular_solve(factor, domain.T, left_side=True, lower=True)
            solved = lax.linalg.triangular_solve(
                factor, middle, left_side=True, lower=True, transpose_a=True
            )
        scores = jnp.dot(sketch, solved, precision=lax.Precision.HIGHEST)
    return (scores, sketch)


def solution(mesh):
    placed = (P(("groups", "ex"), None), P("ex", None), P(), P())
    return jax.shard_map(
        on_device,
        mesh=mesh,
        in_specs=placed,
        out_specs=(P(("groups", "ex"), None), P(("groups", "ex"), None)),
        check_vma=False,
    )
```
